128 devices in a mesh: dom: 8 (over x, z_hi), grid: 16 (over z_lo, y, core).
Axes of the slice: x: 4, y: 4, z: 4 (z_hi: 2, z_lo: 2; z = z_hi * 2 + z_lo), core: 2. Of those that a mesh axis runs over, the one named last changes fastest.
Arguments:
- bands: float32 [8, 4, 64, 48, 1280], P('dom', None, None, 'grid'), may hold values from -6 to 6
- potential: float32 [4, 48, 32, 256], P(None, 'grid', 'dom'), may hold values from -1 to 1
- domain_blocks: int32 [8, 6], replicated, may hold values from 0 to 31, as said below
- block_slots: int32 [32], replicated, may hold values from 0 to 31, as said below
- domain_offsets: int32 [8], replicated, may hold values from 0 to 3
Outputs:
- filtered: float32 [8, 4, 64, 48, 1280], P('dom', None, None, 'grid')
The draws below stay inside these ranges and needn't reach their ends.
Inputs may be any that keep to these rules, and one draw needn't show every extreme that they name: `domain_blocks`: each row is 6 cyclically consecutive logical blocks. `block_slots`: a permutation; slot // 4 is the index of dom that stores the block; no domain has more than 1 of its blocks stored on one index of dom, and some domain has exactly 1.
All inputs are finite; a program needn't handle non-finite values.
Results may differ from the reference program's by a relative error of at most 0.0003.
Values sent between devices are 32-bit elements; how exact they have to be, the bound alone decides.
No kernel may reach another device: no remote copies, remote signals or barrier semaphores. Data moves between devices by JAX's collectives and lax.ppermute only.
A program may use at most 128 MiB of HBM per device.

```python
import jax
import jax.numpy as jnp
from jax import lax

BANDS = 64
BY = 4
DZ = 64
BLK_DEV = 4
OVL = 6
NDOMAINS = 8
NBLK = 32
DX = 48
CELLS = 1280
BCELLS = 256


def draw_domain_blocks(key, part):
    first_key, second_key = jax.random.split(jax.random.fold_in(key, 11))
    starts = jax.random.randint(first_key, (NDOMAINS,), 0, NBLK)
    chosen = jax.random.randint(second_key, (), 0, NDOMAINS)
    starts = jnp.where(jnp.arange(NDOMAINS) == chosen, NBLK - 1, starts)
    return ((starts[:, None] + jnp.arange(OVL)[None, :]) % NBLK).astype(jnp.int32)


def draw_block_slots(key, part):
    first_key, second_key = jax.random.split(jax.random.fold_in(key, 23))
    owners = jax.random.permutation(first_key, NDOMAINS)
    within = jax.random.permutation(second_key, BLK_DEV)
    logical = jnp.arange(NBLK)
    return (owners[logical % NDOMAINS] * BLK_DEV + within[logical // NDOMAINS]).astype(jnp.int32)


def draw_domain_offsets(key, part):
    first_key, second_key, third_key = jax.random.split(jax.random.fold_in(key, 37), 3)
    shifts = jax.random.randint(first_key, (NDOMAINS,), 0, BY)
    high_at = jax.random.randint(second_key, (), 0, NDOMAINS)
    low_at = (high_at + 1 + jax.random.randint(third_key, (), 0, NDOMAINS - 1)) % NDOMAINS
    domain_ids = jnp.arange(NDOMAINS)
    shifts = jnp.where(domain_ids == high_at, BY - 1, shifts)
    shifts = jnp.where(domain_ids == low_at, 0, shifts)
    return shifts.astype(jnp.int32)


def block_levels(key, dims, cuts, smallest, largest):
    def one(axis_at, blocks):
        heights = jax.random.uniform(jax.random.fold_in(jax.random.fold_in(key, 6), axis_at), (blocks,), jnp.float32, smallest / len(cuts), largest / len(cuts))
        return jnp.repeat(jnp.exp(heights), dims[axis_at] // blocks).reshape((-1,) + (1,) * (len(dims) - axis_at - 1))

    loudness = one(*cuts[0])
    for cut in cuts[1:]:
        loudness = loudness * one(*cut)
    return loudness


def normal_values(key, extent, deviation, reach, pieces=(), held_as=jnp.bfloat16):
    result = deviation * jax.random.normal(key, extent, jnp.float32)
    if pieces:
        result = result * block_levels(key, extent, pieces, -0.22, 0.18)
    return jnp.clip(result, -reach, reach).astype(held_as)


def setup_inputs(seed: int = 0) -> dict:
    splits = jax.random.split(jax.random.key(seed), 6)
    return {
        "bands": normal_values(splits[0], (NDOMAINS, 4, BANDS, DX, CELLS), 1.0, 6.0, ((0, 8), (3, 16)), jnp.float32),
        "potential": normal_values(splits[1], (4, DX, NBLK, BCELLS), 0.4, 1.0, ((1, 16), (2, 8)), jnp.float32),
        "domain_blocks": draw_domain_blocks(jax.random.fold_in(splits[5], 71), 0),
        "block_slots": draw_block_slots(jax.random.fold_in(splits[5], 71), 0),
        "domain_offsets": draw_domain_offsets(jax.random.fold_in(splits[5], 71), 0),
    }


e_half = 4.5
centre = 5.0
sigma_one = e_half / (-3.5 - centre)
sigma_two = 1.0 / (2.0 / sigma_one - sigma_one)
sigma_three = 1.0 / (2.0 / sigma_one - sigma_two)
rashba = 0.3


def along(field, steps):
    zeros = jnp.zeros(field.shape[:-1] + (abs(steps),), jnp.float32)
    if steps > 0:
        return jnp.concatenate([field[..., steps:], zeros], axis=-1)
    return jnp.concatenate([zeros, field[..., :steps]], axis=-1)


def apply_h(padded, fields):
    middle = padded[:, :, 1:-1]
    x_next = padded[:, :, 2:]
    x_prev = padded[:, :, :-2]
    cell_ids = jnp.arange(middle.shape[-1]) % DZ
    z_high = (cell_ids != DZ - 1).astype(jnp.float32)
    z_low = (cell_ids != 0).astype(jnp.float32)
    y_next = along(middle, DZ)
    y_prev = along(middle, -DZ)
    z_next = along(middle, 1) * z_high
    z_prev = along(middle, -1) * z_low
    lapl = x_next + x_prev + y_next + y_prev + z_next + z_prev - 6.0 * middle
    diff_x = 0.5 * (x_next - x_prev)
    diff_y = 0.5 * (y_next - y_prev)
    pot_v, mag_x, mag_y, mag_z = fields[0][None], fields[1][None], fields[2][None], fields[3][None]
    a_up, b_up, a_dn, b_dn = middle[0], middle[1], middle[2], middle[3]
    out_a = -0.5 * lapl[0] + pot_v * a_up + mag_z * a_up + mag_x * a_dn + mag_y * b_dn + rashba * (diff_y[3] + diff_x[2])
    out_b = -0.5 * lapl[1] + pot_v * b_up + mag_z * b_up + mag_x * b_dn - mag_y * a_dn + rashba * (diff_x[3] - diff_y[2])
    out_c = -0.5 * lapl[2] + pot_v * a_dn + mag_x * a_up - mag_y * b_up - mag_z * a_dn + rashba * (diff_y[1] - diff_x[0])
    out_d = -0.5 * lapl[3] + pot_v * b_dn + mag_x * b_up + mag_y * a_up - mag_z * b_dn - rashba * (diff_y[0] + diff_x[1])
    return jnp.stack([out_a, out_b, out_c, out_d])


def padded_x(field):
    return jnp.pad(field, ((0, 0), (0, 0), (1, 1), (0, 0)))


def filter_bands(spinors, fields):
    first = (sigma_one / e_half) * (apply_h(padded_x(spinors), fields) - centre * spinors)
    second = (2.0 * sigma_two / e_half) * (apply_h(padded_x(first), fields) - centre * first) - sigma_one * sigma_two * spinors
    third = (2.0 * sigma_three / e_half) * (apply_h(padded_x(second), fields) - centre * second) - sigma_two * sigma_three * first
    return third


def reference(bands, potential, domain_blocks, block_slots, domain_offsets):
    slot_ids = block_slots[domain_blocks]

    def one_domain(inputs):
        block_row, shift_rows, spinors = inputs
        picked = jnp.take(potential, block_row, axis=2)
        window = picked.reshape(4, DX, OVL * BY * DZ)
        fields = lax.dynamic_slice_in_dim(window, (shift_rows * DZ).astype(jnp.int32), CELLS, 2)
        return filter_bands(spinors, fields)

    return lax.map(one_domain, (slot_ids, domain_offsets, bands))
```

```python
import jax
import jax.numpy as jnp
from jax import lax
from jax.experimental import pallas as pl
from jax.experimental.pallas import tpu as pltpu
from jax.sharding import PartitionSpec as P

DZ = 64
OVL = 6
CELLS = 1280
HALO = 3
CHUNK = 16


e_half = 4.5
centre = 5.0
sigma_one = e_half / (-3.5 - centre)
sigma_two = 1.0 / (2.0 / sigma_one - sigma_one)
sigma_three = 1.0 / (2.0 / sigma_one - sigma_two)
rashba = 0.3

ALPHA1 = sigma_one / e_half
ALPHA2 = 2.0 * sigma_two / e_half
BETA2 = -sigma_one * sigma_two
ALPHA3 = 2.0 * sigma_three / e_half
BETA3 = -sigma_two * sigma_three
RH = 0.5 * rashba


def _make_kernel(planes, chunk, aliased):
    rows_n = chunk // 8

    def kernel(valid_ref, f_ref, lo_ref, cur_ref, hi_ref, *rest):
        if aliased:
            out_ref, y1_ref, y2_ref = rest[1:]
        else:
            out_ref, y1_ref, y2_ref = rest
        cell = lax.broadcasted_iota(jnp.int32, (8, CELLS), 1)
        zc = cell % DZ
        m_yn = cell < CELLS - DZ
        m_yp = cell >= DZ
        m_zn = zc != DZ - 1
        m_zp = zc != 0

        def band(q, k, rows):
            if q < 0:
                return lo_ref[k, q + HALO, rows, :]
            if q < planes:
                return cur_ref[k, q, rows, :]
            return hi_ref[k, q - planes, rows, :]

        def from_y1(q, k, rows):
            return y1_ref[k, q + 2, rows, :]

        def from_y2(q, k, rows):
            return y2_ref[k, q + 1, rows, :]

        def apply(src, q, rows):
            d_up = f_ref[0, q + 2 : q + 3, :]
            d_dn = f_ref[1, q + 2 : q + 3, :]
            bx = f_ref[2, q + 2 : q + 3, :]
            by = f_ref[3, q + 2 : q + 3, :]
            o = [None] * 4

            def add(i, v):
                o[i] = v if o[i] is None else o[i] + v

            for k in range(4):
                m = src(q, k, rows)
                xn = src(q + 1, k, rows)
                xp = src(q - 1, k, rows)
                yn = jnp.where(m_yn, pltpu.roll(m, CELLS - DZ, 1), 0.0)
                yp = jnp.where(m_yp, pltpu.roll(m, DZ, 1), 0.0)
                zn = jnp.where(m_zn, pltpu.roll(m, CELLS - 1, 1), 0.0)
                zp = jnp.where(m_zp, pltpu.roll(m, 1, 1), 0.0)
                nb = (xn + xp) + (yn + yp) + (zn + zp)
                dx = RH * (xn - xp)
                dy = RH * (yn - yp)
                if k == 0:
                    add(0, d_up * m - 0.5 * nb)
                    add(2, bx * m - dx)
                    add(3, by * m - dy)
                elif k == 1:
                    add(1, d_up * m - 0.5 * nb)
                    add(2, dy - by * m)
                    add(3, bx * m - dx)
                elif k == 2:
                    add(2, d_dn * m - 0.5 * nb)
                    add(0, bx * m + dx)
                    add(1, -(by * m) - dy)
                else:
                    add(3, d_dn * m - 0.5 * nb)
                    add(0, by * m + dy)
                    add(1, bx * m + dx)
            return o

        def run_stage(src, dst, prev, q_lo, q_hi, alpha, beta):
            for q in range(q_lo, q_hi):
                halo_plane = q < 0 or q >= planes

                def body(r, carry, q=q, halo_plane=halo_plane):
                    rows = pl.ds(pl.multiple_of(r * 8, 8), 8)
                    o = apply(src, q, rows)
                    scale = valid_ref[q + HALO] if halo_plane else None
                    for k in range(4):
                        res = alpha * o[k]
                        if prev is not None:
                            res = res + beta * prev(q, k, rows)
                        if scale is not None:
                            res = res * scale
                        dst(q, k, rows, res)
                    return carry

                lax.fori_loop(0, rows_n, body, 0)

        def put_y1(q, k, rows, v):
            y1_ref[k, q + 2, rows, :] = v

        def put_y2(q, k, rows, v):
            y2_ref[k, q + 1, rows, :] = v

        def put_out(q, k, rows, v):
            out_ref[k, q, rows, :] = v

        run_stage(band, put_y1, None, -2, planes + 2, ALPHA1, 0.0)
        run_stage(from_y1, put_y2, band, -1, planes + 1, ALPHA2, BETA2)
        run_stage(from_y2, put_out, from_y1, 0, planes, ALPHA3, BETA3)

    return kernel


def _filter_chunk(valid, fext, lo, cur_full, hi, acc, c, planes, chunk):
    aliased = acc is not None
    nb_full = cur_full.shape[2]
    blk = (4, HALO, chunk, CELLS)
    in_specs = [
        pl.BlockSpec(memory_space=pltpu.SMEM),
        pl.BlockSpec(fext.shape, lambda i: (0, 0, 0)),
        pl.BlockSpec(blk, lambda i: (0, 0, 0, 0)),
        pl.BlockSpec((4, planes, chunk, CELLS), lambda i: (0, 0, c, 0)),
        pl.BlockSpec(blk, lambda i: (0, 0, 0, 0)),
    ]
    args = [valid, fext, lo, cur_full, hi]
    extra = {}
    if aliased:
        in_specs.append(pl.BlockSpec(memory_space=pl.ANY))
        args.append(acc)
        extra["input_output_aliases"] = {5: 0}
    return pl.pallas_call(
        _make_kernel(planes, chunk, aliased),
        grid=(1,),
        in_specs=in_specs,
        out_specs=pl.BlockSpec((4, planes, chunk, CELLS), lambda i: (0, 0, c, 0)),
        out_shape=jax.ShapeDtypeStruct((4, planes, nb_full, CELLS), jnp.float32),
        scratch_shapes=[
            pltpu.VMEM((4, planes + 4, chunk, CELLS), jnp.float32),
            pltpu.VMEM((4, planes + 2, chunk, CELLS), jnp.float32),
        ],
        compiler_params=pltpu.CompilerParams(vmem_limit_bytes=48 * 1024 * 1024),
        **extra,
    )(*args)


def _shift(x, axis, step):
    count = lax.axis_size(axis)
    if step > 0:
        pairs = [(i, i + 1) for i in range(count - 1)]
    else:
        pairs = [(i + 1, i) for i in range(count - 1)]
    return lax.ppermute(x, axis, pairs)


def _fields(potential, domain_blocks, block_slots, domain_offsets):
    ndom = lax.axis_size("dom")
    per_dev = potential.shape[2]
    planes = potential.shape[1]
    d = lax.axis_index("dom")
    slot_of = block_slots[domain_blocks]

    def local_for(t):
        slots_t = slot_of[t]
        match = (slots_t // per_dev) == d
        return jnp.sum(jnp.where(match, slots_t % per_dev, 0))

    recv = []
    for k in range(ndom):
        t = (d + k) % ndom
        send = lax.dynamic_index_in_dim(potential, local_for(t), axis=2, keepdims=False)
        if k == 0:
            recv.append(send)
        else:
            recv.append(lax.ppermute(send, "dom", [(i, (i + k) % ndom) for i in range(ndom)]))
    allr = jnp.stack(recv)
    mine = slot_of[d]
    ks = (d - mine // per_dev) % ndom
    blocks = jnp.take(allr, ks, axis=0)
    window = jnp.transpose(blocks, (1, 2, 0, 3)).reshape(4, planes, OVL * potential.shape[3])
    f = lax.dynamic_slice_in_dim(window, domain_offsets[d] * DZ, CELLS, 2)
    v, bx, by, bz = f[0], f[1], f[2], f[3]
    return jnp.stack([v + bz + (3.0 - centre), v - bz + (3.0 - centre), bx, by])


def per_device(bands, potential, domain_blocks, block_slots, domain_offsets):
    b = jnp.transpose(bands[0], (0, 2, 1, 3))
    planes = b.shape[1]
    nbands = b.shape[2]
    g = lax.axis_index("grid")
    ng = lax.axis_size("grid")
    chunk = CHUNK

    los, his = [], []
    for c in range(nbands // chunk):
        bc = b[:, :, c * chunk : (c + 1) * chunk]
        los.append(_shift(bc[:, planes - HALO :], "grid", 1))
        his.append(_shift(bc[:, :HALO], "grid", -1))

    f = _fields(potential, domain_blocks, block_slots, domain_offsets)
    f_lo = _shift(f[:, planes - 2 :], "grid", 1)
    f_hi = _shift(f[:, :2], "grid", -1)
    fext = jnp.concatenate([f_lo, f, f_hi], axis=1)

    q = jnp.arange(-HALO, planes + HALO)
    glob = g * planes + q
    valid = ((glob >= 0) & (glob < ng * planes)).astype(jnp.float32)

    acc = None
    for c in range(nbands // chunk):
        acc = _filter_chunk(valid, fext, los[c], b, his[c], acc, c, planes, chunk)
    return jnp.transpose(acc, (0, 2, 1, 3))[None]


def solution(mesh):
    placed = (P("dom", None, None, "grid", None), P(None, "grid", "dom", None), P(), P(), P())
    return jax.shard_map(
        per_device,
        mesh=mesh,
        in_specs=placed,
        out_specs=P("dom", None, None, "grid", None),
        check_vma=False,
    )
```

```python
import jax
import jax.numpy as jnp
from jax import lax
from jax.experimental import pallas as pl
from jax.experimental.pallas import tpu as pltpu
from jax.sharding import PartitionSpec as P

DZ = 64
OVL = 6
CELLS = 1280
HALO = 3
CHUNK = 16


e_half = 4.5
centre = 5.0
sigma_one = e_half / (-3.5 - centre)
sigma_two = 1.0 / (2.0 / sigma_one - sigma_one)
sigma_three = 1.0 / (2.0 / sigma_one - sigma_two)
rashba = 0.3

ALPHA1 = sigma_one / e_half
ALPHA2 = 2.0 * sigma_two / e_half
BETA2 = -sigma_one * sigma_two
ALPHA3 = 2.0 * sigma_three / e_half
BETA3 = -sigma_two * sigma_three
RH = 0.5 * rashba


def _make_kernel(planes, chunk, aliased):
    rows_n = chunk // 8

    def kernel(valid_ref, f_ref, lo_ref, cur_ref, hi_ref, *rest):
        if aliased:
            out_ref, y1_ref, y2_ref = rest[1:]
        else:
            out_ref, y1_ref, y2_ref = rest
        cell = lax.broadcasted_iota(jnp.int32, (8, CELLS), 1)
        zc = cell % DZ
        m_yn = cell < CELLS - DZ
        m_yp = cell >= DZ
        m_zn = zc != DZ - 1
        m_zp = zc != 0

        def band(q, k, rows):
            if q < 0:
                return lo_ref[k, q + HALO, rows, :]
            if q < planes:
                return cur_ref[k, q, rows, :]
            return hi_ref[k, q - planes, rows, :]

        def from_y1(q, k, rows):
            return y1_ref[k, q + 2, rows, :]

        def from_y2(q, k, rows):
            return y2_ref[k, q + 1, rows, :]

        def apply(src, q, rows):
            d_up = f_ref[0, q + 2 : q + 3, :]
            d_dn = f_ref[1, q + 2 : q + 3, :]
            bx = f_ref[2, q + 2 : q + 3, :]
            by = f_ref[3, q + 2 : q + 3, :]
            o = [None] * 4

            def add(i, v):
                o[i] = v if o[i] is None else o[i] + v

            for k in range(4):
                m = src(q, k, rows)
                xn = src(q + 1, k, rows)
                xp = src(q - 1, k, rows)
                yn = jnp.where(m_yn, pltpu.roll(m, CELLS - DZ, 1), 0.0)
                yp = jnp.where(m_yp, pltpu.roll(m, DZ, 1), 0.0)
                zn = jnp.where(m_zn, pltpu.roll(m, CELLS - 1, 1), 0.0)
                zp = jnp.where(m_zp, pltpu.roll(m, 1, 1), 0.0)
                nb = (xn + xp) + (yn + yp) + (zn + zp)
                dx = RH * (xn - xp)
                dy = RH * (yn - yp)
                if k == 0:
                    add(0, d_up * m - 0.5 * nb)
                    add(2, bx * m - dx)
                    add(3, by * m - dy)
                elif k == 1:
                    add(1, d_up * m - 0.5 * nb)
                    add(2, dy - by * m)
                    add(3, bx * m - dx)
                elif k == 2:
                    add(2, d_dn * m - 0.5 * nb)
                    add(0, bx * m + dx)
                    add(1, -(by * m) - dy)
                else:
                    add(3, d_dn * m - 0.5 * nb)
                    add(0, by * m + dy)
                    add(1, bx * m + dx)
            return o

        def run_stage(src, dst, prev, q_lo, q_hi, alpha, beta):
            for q in range(q_lo, q_hi):
                halo_plane = q < 0 or q >= planes

                def body(r, carry, q=q, halo_plane=halo_plane):
                    rows = pl.ds(pl.multiple_of(r * 8, 8), 8)
                    o = apply(src, q, rows)
                    scale = valid_ref[q + HALO] if halo_plane else None
                    for k in range(4):
                        res = alpha * o[k]
                        if prev is not None:
                            res = res + beta * prev(q, k, rows)
                        if scale is not None:
                            res = res * scale
                        dst(q, k, rows, res)
                    return carry

                lax.fori_loop(0, rows_n, body, 0)

        def put_y1(q, k, rows, v):
            y1_ref[k, q + 2, rows, :] = v

        def put_y2(q, k, rows, v):
            y2_ref[k, q + 1, rows, :] = v

        def put_out(q, k, rows, v):
            out_ref[k, q, rows, :] = v

        run_stage(band, put_y1, None, -2, planes + 2, ALPHA1, 0.0)
        run_stage(from_y1, put_y2, band, -1, planes + 1, ALPHA2, BETA2)
        run_stage(from_y2, put_out, from_y1, 0, planes, ALPHA3, BETA3)

    return kernel


def _filter_chunk(valid, fext, lo, cur_full, hi, acc, c, planes, chunk):
    aliased = acc is not None
    nb_full = cur_full.shape[2]
    blk = (4, HALO, chunk, CELLS)
    in_specs = [
        pl.BlockSpec(memory_space=pltpu.SMEM),
        pl.BlockSpec(fext.shape, lambda i: (0, 0, 0)),
        pl.BlockSpec(blk, lambda i: (0, 0, 0, 0)),
        pl.BlockSpec((4, planes, chunk, CELLS), lambda i: (0, 0, c, 0)),
        pl.BlockSpec(blk, lambda i: (0, 0, 0, 0)),
    ]
    args = [valid, fext, lo, cur_full, hi]
    extra = {}
    if aliased:
        in_specs.append(pl.BlockSpec(memory_space=pl.ANY))
        args.append(acc)
        extra["input_output_aliases"] = {5: 0}
    return pl.pallas_call(
        _make_kernel(planes, chunk, aliased),
        grid=(1,),
        in_specs=in_specs,
        out_specs=pl.BlockSpec((4, planes, chunk, CELLS), lambda i: (0, 0, c, 0)),
        out_shape=jax.ShapeDtypeStruct((4, planes, nb_full, CELLS), jnp.float32),
        scratch_shapes=[
            pltpu.VMEM((4, planes + 4, chunk, CELLS), jnp.float32),
            pltpu.VMEM((4, planes + 2, chunk, CELLS), jnp.float32),
        ],
        compiler_params=pltpu.CompilerParams(vmem_limit_bytes=48 * 1024 * 1024),
        **extra,
    )(*args)


def _shift(x, axis, step):
    count = lax.axis_size(axis)
    if step > 0:
        pairs = [(i, i + 1) for i in range(count - 1)]
    else:
        pairs = [(i + 1, i) for i in range(count - 1)]
    return lax.ppermute(x, axis, pairs)


def _fields(potential, domain_blocks, block_slots, domain_offsets):
    ndom = lax.axis_size("dom")
    per_dev = potential.shape[2]
    planes = potential.shape[1]
    d = lax.axis_index("dom")
    slot_of = block_slots[domain_blocks]

    def local_for(t):
        slots_t = slot_of[t]
        match = (slots_t // per_dev) == d
        return jnp.sum(jnp.where(match, slots_t % per_dev, 0))

    sends = []
    for t in range(ndom):
        sends.append(lax.dynamic_index_in_dim(potential, local_for(t), axis=2, keepdims=False))
    allr = lax.all_to_all(jnp.stack(sends), "dom", 0, 0, tiled=True)
    mine = slot_of[d]
    blocks = jnp.take(allr, mine // per_dev, axis=0)
    window = jnp.transpose(blocks, (1, 2, 0, 3)).reshape(4, planes, OVL * potential.shape[3])
    f = lax.dynamic_slice_in_dim(window, domain_offsets[d] * DZ, CELLS, 2)
    v, bx, by, bz = f[0], f[1], f[2], f[3]
    return jnp.stack([v + bz + (3.0 - centre), v - bz + (3.0 - centre), bx, by])


def per_device(bands, potential, domain_blocks, block_slots, domain_offsets):
    b = jnp.transpose(bands[0], (0, 2, 1, 3))
    planes = b.shape[1]
    nbands = b.shape[2]
    g = lax.axis_index("grid")
    ng = lax.axis_size("grid")
    chunk = CHUNK

    los, his = [], []
    for c in range(nbands // chunk):
        bc = b[:, :, c * chunk : (c + 1) * chunk]
        los.append(_shift(bc[:, planes - HALO :], "grid", 1))
        his.append(_shift(bc[:, :HALO], "grid", -1))

    f = _fields(potential, domain_blocks, block_slots, domain_offsets)
    f_lo = _shift(f[:, planes - 2 :], "grid", 1)
    f_hi = _shift(f[:, :2], "grid", -1)
    fext = jnp.concatenate([f_lo, f, f_hi], axis=1)

    q = jnp.arange(-HALO, planes + HALO)
    glob = g * planes + q
    valid = ((glob >= 0) & (glob < ng * planes)).astype(jnp.float32)

    acc = None
    for c in range(nbands // chunk):
        acc = _filter_chunk(valid, fext, los[c], b, his[c], acc, c, planes, chunk)
    return jnp.transpose(acc, (0, 2, 1, 3))[None]


def solution(mesh):
    placed = (P("dom", None, None, "grid", None), P(None, "grid", "dom", None), P(), P(), P())
    return jax.shard_map(
        per_device,
        mesh=mesh,
        in_specs=placed,
        out_specs=P("dom", None, None, "grid", None),
        check_vma=False,
    )
```

```python
import jax
import jax.numpy as jnp
from jax import lax
from jax.experimental import pallas as pl
from jax.experimental.pallas import tpu as pltpu
from jax.sharding import PartitionSpec as P

DZ = 64
OVL = 6
CELLS = 1280
HALO = 3
CHUNK = 16


e_half = 4.5
centre = 5.0
sigma_one = e_half / (-3.5 - centre)
sigma_two = 1.0 / (2.0 / sigma_one - sigma_one)
sigma_three = 1.0 / (2.0 / sigma_one - sigma_two)
rashba = 0.3

ALPHA1 = sigma_one / e_half
ALPHA2 = 2.0 * sigma_two / e_half
BETA2 = -sigma_one * sigma_two
ALPHA3 = 2.0 * sigma_three / e_half
BETA3 = -sigma_two * sigma_three
RH = 0.5 * rashba


def _make_kernel(planes, chunk, aliased):
    rows_n = chunk // 8

    def kernel(valid_ref, f_ref, lo_ref, cur_ref, hi_ref, *rest):
        if aliased:
            out_ref, y1_ref, y2_ref = rest[1:]
        else:
            out_ref, y1_ref, y2_ref = rest
        cell = lax.broadcasted_iota(jnp.int32, (8, CELLS), 1)
        zc = cell % DZ
        m_yn = cell < CELLS - DZ
        m_yp = cell >= DZ
        m_zn = zc != DZ - 1
        m_zp = zc != 0

        def band(q, k, rows):
            if q < 0:
                return lo_ref[k, q + HALO, rows, :]
            if q < planes:
                return cur_ref[k, q, rows, :]
            return hi_ref[k, q - planes, rows, :]

        def from_y1(q, k, rows):
            return y1_ref[k, q + 2, rows, :]

        def from_y2(q, k, rows):
            return y2_ref[k, q + 1, rows, :]

        def apply(src, q, rows):
            d_up = f_ref[0, q + 2 : q + 3, :]
            d_dn = f_ref[1, q + 2 : q + 3, :]
            bx = f_ref[2, q + 2 : q + 3, :]
            by = f_ref[3, q + 2 : q + 3, :]
            o = [None] * 4

            def add(i, v):
                o[i] = v if o[i] is None else o[i] + v

            for k in range(4):
                m = src(q, k, rows)
                xn = src(q + 1, k, rows)
                xp = src(q - 1, k, rows)
                yn = jnp.where(m_yn, pltpu.roll(m, CELLS - DZ, 1), 0.0)
                yp = jnp.where(m_yp, pltpu.roll(m, DZ, 1), 0.0)
                zn = jnp.where(m_zn, pltpu.roll(m, CELLS - 1, 1), 0.0)
                zp = jnp.where(m_zp, pltpu.roll(m, 1, 1), 0.0)
                nb = (xn + xp) + (yn + yp) + (zn + zp)
                dx = RH * (xn - xp)
                dy = RH * (yn - yp)
                if k == 0:
                    add(0, d_up * m - 0.5 * nb)
                    add(2, bx * m - dx)
                    add(3, by * m - dy)
                elif k == 1:
                    add(1, d_up * m - 0.5 * nb)
                    add(2, dy - by * m)
                    add(3, bx * m - dx)
                elif k == 2:
                    add(2, d_dn * m - 0.5 * nb)
                    add(0, bx * m + dx)
                    add(1, -(by * m) - dy)
                else:
                    add(3, d_dn * m - 0.5 * nb)
                    add(0, by * m + dy)
                    add(1, bx * m + dx)
            return o

        def run_stage(src, dst, prev, q_lo, q_hi, alpha, beta):
            for q in range(q_lo, q_hi):
                halo_plane = q < 0 or q >= planes

                def body(r, carry, q=q, halo_plane=halo_plane):
                    rows = pl.ds(pl.multiple_of(r * 8, 8), 8)
                    o = apply(src, q, rows)
                    scale = valid_ref[q + HALO] if halo_plane else None
                    for k in range(4):
                        res = alpha * o[k]
                        if prev is not None:
                            res = res + beta * prev(q, k, rows)
                        if scale is not None:
                            res = res * scale
                        dst(q, k, rows, res)
                    return carry

                lax.fori_loop(0, rows_n, body, 0)

        def put_y1(q, k, rows, v):
            y1_ref[k, q + 2, rows, :] = v

        def put_y2(q, k, rows, v):
            y2_ref[k, q + 1, rows, :] = v

        def put_out(q, k, rows, v):
            out_ref[k, q, rows, :] = v

        run_stage(band, put_y1, None, -2, planes + 2, ALPHA1, 0.0)
        run_stage(from_y1, put_y2, band, -1, planes + 1, ALPHA2, BETA2)
        run_stage(from_y2, put_out, from_y1, 0, planes, ALPHA3, BETA3)

    return kernel


def _filter_chunk(valid, fext, lo, cur_full, hi, acc, c, planes, chunk):
    aliased = acc is not None
    nb_full = cur_full.shape[2]
    blk = (4, HALO, chunk, CELLS)
    in_specs = [
        pl.BlockSpec(memory_space=pltpu.SMEM),
        pl.BlockSpec(fext.shape, lambda i: (0, 0, 0)),
        pl.BlockSpec(blk, lambda i: (0, 0, 0, 0)),
        pl.BlockSpec((4, planes, chunk, CELLS), lambda i: (0, 0, c, 0)),
        pl.BlockSpec(blk, lambda i: (0, 0, 0, 0)),
    ]
    args = [valid, fext, lo, cur_full, hi]
    extra = {}
    if aliased:
        in_specs.append(pl.BlockSpec(memory_space=pl.ANY))
        args.append(acc)
        extra["input_output_aliases"] = {5: 0}
    return pl.pallas_call(
        _make_kernel(planes, chunk, aliased),
        grid=(1,),
        in_specs=in_specs,
        out_specs=pl.BlockSpec((4, planes, chunk, CELLS), lambda i: (0, 0, c, 0)),
        out_shape=jax.ShapeDtypeStruct((4, planes, nb_full, CELLS), jnp.float32),
        scratch_shapes=[
            pltpu.VMEM((4, planes + 4, chunk, CELLS), jnp.float32),
            pltpu.VMEM((4, planes + 2, chunk, CELLS), jnp.float32),
        ],
        compiler_params=pltpu.CompilerParams(vmem_limit_bytes=48 * 1024 * 1024),
        **extra,
    )(*args)


def _shift(x, axis, step):
    count = lax.axis_size(axis)
    if step > 0:
        pairs = [(i, i + 1) for i in range(count - 1)]
    else:
        pairs = [(i + 1, i) for i in range(count - 1)]
    return lax.ppermute(x, axis, pairs)


def _fields(potential, domain_blocks, block_slots, domain_offsets):
    ndom = lax.axis_size("dom")
    per_dev = potential.shape[2]
    planes = potential.shape[1]
    d = lax.axis_index("dom")
    slot_of = block_slots[domain_blocks]

    def local_for(t):
        slots_t = slot_of[t]
        match = (slots_t // per_dev) == d
        return jnp.sum(jnp.where(match, slots_t % per_dev, 0))

    locs = jnp.stack([local_for(t) for t in range(ndom)])
    sends = jnp.moveaxis(jnp.take(potential, locs, axis=2), 2, 0)
    allr = lax.all_to_all(sends, "dom", 0, 0, tiled=True)
    mine = slot_of[d]
    blocks = jnp.take(allr, mine // per_dev, axis=0)
    window = jnp.transpose(blocks, (1, 2, 0, 3)).reshape(4, planes, OVL * potential.shape[3])
    f = lax.dynamic_slice_in_dim(window, domain_offsets[d] * DZ, CELLS, 2)
    v, bx, by, bz = f[0], f[1], f[2], f[3]
    return jnp.stack([v + bz + (3.0 - centre), v - bz + (3.0 - centre), bx, by])


def per_device(bands, potential, domain_blocks, block_slots, domain_offsets):
    b = jnp.transpose(bands[0], (0, 2, 1, 3))
    planes = b.shape[1]
    nbands = b.shape[2]
    g = lax.axis_index("grid")
    ng = lax.axis_size("grid")
    chunk = CHUNK

    f = _fields(potential, domain_blocks, block_slots, domain_offsets)
    f_lo = _shift(f[:, planes - 2 :], "grid", 1)
    f_hi = _shift(f[:, :2], "grid", -1)
    fext = jnp.concatenate([f_lo, f, f_hi], axis=1)
    b, fext = lax.optimization_barrier((b, fext))

    los, his = [], []
    for c in range(nbands // chunk):
        bc = b[:, :, c * chunk : (c + 1) * chunk]
        los.append(_shift(bc[:, planes - HALO :], "grid", 1))
        his.append(_shift(bc[:, :HALO], "grid", -1))

    q = jnp.arange(-HALO, planes + HALO)
    glob = g * planes + q
    valid = ((glob >= 0) & (glob < ng * planes)).astype(jnp.float32)

    acc = None
    for c in range(nbands // chunk):
        acc = _filter_chunk(valid, fext, los[c], b, his[c], acc, c, planes, chunk)
    return jnp.transpose(acc, (0, 2, 1, 3))[None]


def solution(mesh):
    placed = (P("dom", None, None, "grid", None), P(None, "grid", "dom", None), P(), P(), P())
    return jax.shard_map(
        per_device,
        mesh=mesh,
        in_specs=placed,
        out_specs=P("dom", None, None, "grid", None),
        check_vma=False,
    )
```

```python
import jax
import jax.numpy as jnp
from jax import lax
from jax.experimental import pallas as pl
from jax.experimental.pallas import tpu as pltpu
from jax.sharding import PartitionSpec as P

DZ = 64
OVL = 6
CELLS = 1280
HALO = 3
CHUNK = 16


e_half = 4.5
centre = 5.0
sigma_one = e_half / (-3.5 - centre)
sigma_two = 1.0 / (2.0 / sigma_one - sigma_one)
sigma_three = 1.0 / (2.0 / sigma_one - sigma_two)
rashba = 0.3

ALPHA1 = sigma_one / e_half
ALPHA2 = 2.0 * sigma_two / e_half
BETA2 = -sigma_one * sigma_two
ALPHA3 = 2.0 * sigma_three / e_half
BETA3 = -sigma_two * sigma_three
RH = 0.5 * rashba


def _make_kernel(planes, chunk, aliased):
    rows_n = chunk // 8

    def kernel(valid_ref, f_ref, lo_ref, cur_ref, hi_ref, *rest):
        if aliased:
            out_ref, y1_ref, y2_ref = rest[1:]
        else:
            out_ref, y1_ref, y2_ref = rest
        cell = lax.broadcasted_iota(jnp.int32, (8, CELLS), 1)
        zc = cell % DZ
        m_yn = cell < CELLS - DZ
        m_yp = cell >= DZ
        m_zn = zc != DZ - 1
        m_zp = zc != 0

        def band(q, k, rows):
            if q < 0:
                return lo_ref[k, q + HALO, rows, :]
            if q < planes:
                return cur_ref[k, q, rows, :]
            return hi_ref[k, q - planes, rows, :]

        def from_y1(q, k, rows):
            return y1_ref[k, q + 2, rows, :]

        def from_y2(q, k, rows):
            return y2_ref[k, q + 1, rows, :]

        def apply(src, q, rows):
            d_up = f_ref[0, q + 2 : q + 3, :]
            d_dn = f_ref[1, q + 2 : q + 3, :]
            bx = f_ref[2, q + 2 : q + 3, :]
            by = f_ref[3, q + 2 : q + 3, :]
            o = [None] * 4

            def add(i, v):
                o[i] = v if o[i] is None else o[i] + v

            for k in range(4):
                m = src(q, k, rows)
                xn = src(q + 1, k, rows)
                xp = src(q - 1, k, rows)
                yn = jnp.where(m_yn, pltpu.roll(m, CELLS - DZ, 1), 0.0)
                yp = jnp.where(m_yp, pltpu.roll(m, DZ, 1), 0.0)
                zn = jnp.where(m_zn, pltpu.roll(m, CELLS - 1, 1), 0.0)
                zp = jnp.where(m_zp, pltpu.roll(m, 1, 1), 0.0)
                nb = (xn + xp) + (yn + yp) + (zn + zp)
                dx = RH * (xn - xp)
                dy = RH * (yn - yp)
                if k == 0:
                    add(0, d_up * m - 0.5 * nb)
                    add(2, bx * m - dx)
                    add(3, by * m - dy)
                elif k == 1:
                    add(1, d_up * m - 0.5 * nb)
                    add(2, dy - by * m)
                    add(3, bx * m - dx)
                elif k == 2:
                    add(2, d_dn * m - 0.5 * nb)
                    add(0, bx * m + dx)
                    add(1, -(by * m) - dy)
                else:
                    add(3, d_dn * m - 0.5 * nb)
                    add(0, by * m + dy)
                    add(1, bx * m + dx)
            return o

        def run_stage(src, dst, prev, q_lo, q_hi, alpha, beta):
            for q in range(q_lo, q_hi):
                halo_plane = q < 0 or q >= planes

                def body(r, carry, q=q, halo_plane=halo_plane):
                    rows = pl.ds(pl.multiple_of(r * 8, 8), 8)
                    o = apply(src, q, rows)
                    scale = valid_ref[q + HALO] if halo_plane else None
                    for k in range(4):
                        res = alpha * o[k]
                        if prev is not None:
                            res = res + beta * prev(q, k, rows)
                        if scale is not None:
                            res = res * scale
                        dst(q, k, rows, res)
                    return carry

                lax.fori_loop(0, rows_n, body, 0)

        def put_y1(q, k, rows, v):
            y1_ref[k, q + 2, rows, :] = v

        def put_y2(q, k, rows, v):
            y2_ref[k, q + 1, rows, :] = v

        def put_out(q, k, rows, v):
            out_ref[k, q, rows, :] = v

        run_stage(band, put_y1, None, -2, planes + 2, ALPHA1, 0.0)
        run_stage(from_y1, put_y2, band, -1, planes + 1, ALPHA2, BETA2)
        run_stage(from_y2, put_out, from_y1, 0, planes, ALPHA3, BETA3)

    return kernel


def _filter_chunk(valid, fext, lo, cur_full, hi, acc, c, planes, chunk):
    aliased = acc is not None
    nb_full = cur_full.shape[2]
    blk = (4, HALO, chunk, CELLS)
    in_specs = [
        pl.BlockSpec(memory_space=pltpu.SMEM),
        pl.BlockSpec(fext.shape, lambda i: (0, 0, 0)),
        pl.BlockSpec(blk, lambda i: (0, 0, 0, 0)),
        pl.BlockSpec((4, planes, chunk, CELLS), lambda i: (0, 0, c, 0)),
        pl.BlockSpec(blk, lambda i: (0, 0, 0, 0)),
    ]
    args = [valid, fext, lo, cur_full, hi]
    extra = {}
    if aliased:
        in_specs.append(pl.BlockSpec(memory_space=pl.ANY))
        args.append(acc)
        extra["input_output_aliases"] = {5: 0}
    return pl.pallas_call(
        _make_kernel(planes, chunk, aliased),
        grid=(1,),
        in_specs=in_specs,
        out_specs=pl.BlockSpec((4, planes, chunk, CELLS), lambda i: (0, 0, c, 0)),
        out_shape=jax.ShapeDtypeStruct((4, planes, nb_full, CELLS), jnp.float32),
        scratch_shapes=[
            pltpu.VMEM((4, planes + 4, chunk, CELLS), jnp.float32),
            pltpu.VMEM((4, planes + 2, chunk, CELLS), jnp.float32),
        ],
        compiler_params=pltpu.CompilerParams(vmem_limit_bytes=48 * 1024 * 1024),
        **extra,
    )(*args)


def _shift(x, axis, step):
    count = lax.axis_size(axis)
    if step > 0:
        pairs = [(i, i + 1) for i in range(count - 1)]
    else:
        pairs = [(i + 1, i) for i in range(count - 1)]
    return lax.ppermute(x, axis, pairs)


def _fields(potential, domain_blocks, block_slots, domain_offsets):
    ndom = lax.axis_size("dom")
    per_dev = potential.shape[2]
    d = lax.axis_index("dom")
    pot = jnp.concatenate(
        [_shift(potential[:, -2:], "grid", 1), potential, _shift(potential[:, :2], "grid", -1)], axis=1
    )
    planes = pot.shape[1]
    slot_of = block_slots[domain_blocks]
    owner = slot_of // per_dev
    locs = jnp.sum(jnp.where(owner == d, slot_of % per_dev, 0), axis=1)
    sends = jnp.moveaxis(jnp.take(pot, locs, axis=2), 2, 0)
    allr = lax.all_to_all(sends, "dom", 0, 0, tiled=True)
    blocks = jnp.take(allr, lax.dynamic_index_in_dim(owner, d, 0, keepdims=False), axis=0)
    window = jnp.transpose(blocks, (1, 2, 0, 3)).reshape(4, planes, OVL * pot.shape[3])
    f = lax.dynamic_slice_in_dim(window, domain_offsets[d] * DZ, CELLS, 2)
    v, bx, by, bz = f[0], f[1], f[2], f[3]
    return jnp.stack([v + bz + (3.0 - centre), v - bz + (3.0 - centre), bx, by])


def per_device(bands, potential, domain_blocks, block_slots, domain_offsets):
    b = jnp.transpose(bands[0], (0, 2, 1, 3))
    planes = b.shape[1]
    nbands = b.shape[2]
    g = lax.axis_index("grid")
    ng = lax.axis_size("grid")
    chunk = CHUNK

    fext = _fields(potential, domain_blocks, block_slots, domain_offsets)
    b, fext = lax.optimization_barrier((b, fext))

    los, his = [], []
    for c in range(nbands // chunk):
        bc = b[:, :, c * chunk : (c + 1) * chunk]
        los.append(_shift(bc[:, planes - HALO :], "grid", 1))
        his.append(_shift(bc[:, :HALO], "grid", -1))

    q = jnp.arange(-HALO, planes + HALO)
    glob = g * planes + q
    valid = ((glob >= 0) & (glob < ng * planes)).astype(jnp.float32)

    acc = None
    for c in range(nbands // chunk):
        acc = _filter_chunk(valid, fext, los[c], b, his[c], acc, c, planes, chunk)
    return jnp.transpose(acc, (0, 2, 1, 3))[None]


def solution(mesh):
    placed = (P("dom", None, None, "grid", None), P(None, "grid", "dom", None), P(), P(), P())
    return jax.shard_map(
        per_device,
        mesh=mesh,
        in_specs=placed,
        out_specs=P("dom", None, None, "grid", None),
        check_vma=False,
    )
```

```python
import jax
import jax.numpy as jnp
from jax import lax
from jax.experimental import pallas as pl
from jax.experimental.pallas import tpu as pltpu
from jax.sharding import PartitionSpec as P

DZ = 64
OVL = 6
CELLS = 1280
HALO = 3
CHUNK = 16


e_half = 4.5
centre = 5.0
sigma_one = e_half / (-3.5 - centre)
sigma_two = 1.0 / (2.0 / sigma_one - sigma_one)
sigma_three = 1.0 / (2.0 / sigma_one - sigma_two)
rashba = 0.3

ALPHA1 = sigma_one / e_half
ALPHA2 = 2.0 * sigma_two / e_half
BETA2 = -sigma_one * sigma_two
ALPHA3 = 2.0 * sigma_three / e_half
BETA3 = -sigma_two * sigma_three
RH = 0.5 * rashba


def _make_kernel(planes, chunk, aliased):
    rows_n = chunk // 8

    def kernel(valid_ref, f_ref, lo_ref, cur_ref, hi_ref, *rest):
        if aliased:
            out_ref, y1_ref, y2_ref = rest[1:]
        else:
            out_ref, y1_ref, y2_ref = rest
        cell = lax.broadcasted_iota(jnp.int32, (8, CELLS), 1)
        zc = cell % DZ
        m_yn = cell < CELLS - DZ
        m_yp = cell >= DZ
        m_zn = zc != DZ - 1
        m_zp = zc != 0

        def band(q, k, rows):
            if q < 0:
                return lo_ref[k, q + HALO, rows, :]
            if q < planes:
                return cur_ref[k, q, rows, :]
            return hi_ref[k, q - planes, rows, :]

        def from_y1(q, k, rows):
            return y1_ref[k, q + 2, rows, :]

        def from_y2(q, k, rows):
            return y2_ref[k, q + 1, rows, :]

        def apply(src, q, rows):
            d_up = f_ref[0, q + 2 : q + 3, :]
            d_dn = f_ref[1, q + 2 : q + 3, :]
            bx = f_ref[2, q + 2 : q + 3, :]
            by = f_ref[3, q + 2 : q + 3, :]
            o = [None] * 4

            def add(i, v):
                o[i] = v if o[i] is None else o[i] + v

            for k in range(4):
                m = src(q, k, rows)
                xn = src(q + 1, k, rows)
                xp = src(q - 1, k, rows)
                yn = jnp.where(m_yn, pltpu.roll(m, CELLS - DZ, 1), 0.0)
                yp = jnp.where(m_yp, pltpu.roll(m, DZ, 1), 0.0)
                zn = jnp.where(m_zn, pltpu.roll(m, CELLS - 1, 1), 0.0)
                zp = jnp.where(m_zp, pltpu.roll(m, 1, 1), 0.0)
                nb = (xn + xp) + (yn + yp) + (zn + zp)
                dx = RH * (xn - xp)
                dy = RH * (yn - yp)
                if k == 0:
                    add(0, d_up * m - 0.5 * nb)
                    add(2, bx * m - dx)
                    add(3, by * m - dy)
                elif k == 1:
                    add(1, d_up * m - 0.5 * nb)
                    add(2, dy - by * m)
                    add(3, bx * m - dx)
                elif k == 2:
                    add(2, d_dn * m - 0.5 * nb)
                    add(0, bx * m + dx)
                    add(1, -(by * m) - dy)
                else:
                    add(3, d_dn * m - 0.5 * nb)
                    add(0, by * m + dy)
                    add(1, bx * m + dx)
            return o

        def run_stage(src, dst, prev, q_lo, q_hi, alpha, beta):
            for q in range(q_lo, q_hi):
                halo_plane = q < 0 or q >= planes

                def body(r, carry, q=q, halo_plane=halo_plane):
                    rows = pl.ds(pl.multiple_of(r * 8, 8), 8)
                    o = apply(src, q, rows)
                    scale = valid_ref[q + HALO] if halo_plane else None
                    for k in range(4):
                        res = alpha * o[k]
                        if prev is not None:
                            res = res + beta * prev(q, k, rows)
                        if scale is not None:
                            res = res * scale
                        dst(q, k, rows, res)
                    return carry

                lax.fori_loop(0, rows_n, body, 0)

        def put_y1(q, k, rows, v):
            y1_ref[k, q + 2, rows, :] = v

        def put_y2(q, k, rows, v):
            y2_ref[k, q + 1, rows, :] = v

        def put_out(q, k, rows, v):
            out_ref[k, q, rows, :] = v

        run_stage(band, put_y1, None, -2, planes + 2, ALPHA1, 0.0)
        run_stage(from_y1, put_y2, band, -1, planes + 1, ALPHA2, BETA2)
        run_stage(from_y2, put_out, from_y1, 0, planes, ALPHA3, BETA3)

    return kernel


def _filter_chunk(valid, fext, lo, cur_full, hi, acc, c, planes, chunk):
    aliased = acc is not None
    nb_full = cur_full.shape[2]
    blk = (4, HALO, chunk, CELLS)
    in_specs = [
        pl.BlockSpec(memory_space=pltpu.SMEM),
        pl.BlockSpec(fext.shape, lambda i: (0, 0, 0)),
        pl.BlockSpec(blk, lambda i: (0, 0, 0, 0)),
        pl.BlockSpec((4, planes, chunk, CELLS), lambda i: (0, 0, c, 0)),
        pl.BlockSpec(blk, lambda i: (0, 0, 0, 0)),
    ]
    args = [valid, fext, lo, cur_full, hi]
    extra = {}
    if aliased:
        in_specs.append(pl.BlockSpec(memory_space=pl.ANY))
        args.append(acc)
        extra["input_output_aliases"] = {5: 0}
    return pl.pallas_call(
        _make_kernel(planes, chunk, aliased),
        grid=(1,),
        in_specs=in_specs,
        out_specs=pl.BlockSpec((4, planes, chunk, CELLS), lambda i: (0, 0, c, 0)),
        out_shape=jax.ShapeDtypeStruct((4, planes, nb_full, CELLS), jnp.float32),
        scratch_shapes=[
            pltpu.VMEM((4, planes + 4, chunk, CELLS), jnp.float32),
            pltpu.VMEM((4, planes + 2, chunk, CELLS), jnp.float32),
        ],
        compiler_params=pltpu.CompilerParams(vmem_limit_bytes=48 * 1024 * 1024),
        **extra,
    )(*args)


def _shift(x, axis, step):
    count = lax.axis_size(axis)
    if step > 0:
        pairs = [(i, i + 1) for i in range(count - 1)]
    else:
        pairs = [(i + 1, i) for i in range(count - 1)]
    return lax.ppermute(x, axis, pairs)


def _fields(potential, domain_blocks, block_slots, domain_offsets, held):
    ndom = lax.axis_size("dom")
    per_dev = potential.shape[2]
    d = lax.axis_index("dom")
    pot = jnp.concatenate(
        [_shift(potential[:, -2:], "grid", 1), potential, _shift(potential[:, :2], "grid", -1)], axis=1
    )
    planes = pot.shape[1]
    slot_of = block_slots[domain_blocks]
    owner = slot_of // per_dev
    locs = jnp.sum(jnp.where(owner == d, slot_of % per_dev, 0), axis=1)
    sends = jnp.moveaxis(jnp.take(pot, locs, axis=2), 2, 0)
    sends, held = lax.optimization_barrier((sends, held))
    allr = lax.all_to_all(sends, "dom", 0, 0, tiled=True)
    blocks = jnp.take(allr, lax.dynamic_index_in_dim(owner, d, 0, keepdims=False), axis=0)
    window = jnp.transpose(blocks, (1, 2, 0, 3)).reshape(4, planes, OVL * pot.shape[3])
    f = lax.dynamic_slice_in_dim(window, domain_offsets[d] * DZ, CELLS, 2)
    v, bx, by, bz = f[0], f[1], f[2], f[3]
    return jnp.stack([v + bz + (3.0 - centre), v - bz + (3.0 - centre), bx, by]), held


def per_device(bands, potential, domain_blocks, block_slots, domain_offsets):
    b = jnp.transpose(bands[0], (0, 2, 1, 3))
    planes = b.shape[1]
    nbands = b.shape[2]
    g = lax.axis_index("grid")
    ng = lax.axis_size("grid")
    chunk = CHUNK

    fext, b = _fields(potential, domain_blocks, block_slots, domain_offsets, b)

    los, his = [], []
    for c in range(nbands // chunk):
        bc = b[:, :, c * chunk : (c + 1) * chunk]
        los.append(_shift(bc[:, planes - HALO :], "grid", 1))
        his.append(_shift(bc[:, :HALO], "grid", -1))

    q = jnp.arange(-HALO, planes + HALO)
    glob = g * planes + q
    valid = ((glob >= 0) & (glob < ng * planes)).astype(jnp.float32)

    acc = None
    for c in range(nbands // chunk):
        acc = _filter_chunk(valid, fext, los[c], b, his[c], acc, c, planes, chunk)
    return jnp.transpose(acc, (0, 2, 1, 3))[None]


def solution(mesh):
    placed = (P("dom", None, None, "grid", None), P(None, "grid", "dom", None), P(), P(), P())
    return jax.shard_map(
        per_device,
        mesh=mesh,
        in_specs=placed,
        out_specs=P("dom", None, None, "grid", None),
        check_vma=False,
    )
```

```python
import jax
import jax.numpy as jnp
from jax import lax
from jax.experimental import pallas as pl
from jax.experimental.pallas import tpu as pltpu
from jax.sharding import PartitionSpec as P

DZ = 64
OVL = 6
CELLS = 1280
HALO = 3
CHUNK = 16


e_half = 4.5
centre = 5.0
sigma_one = e_half / (-3.5 - centre)
sigma_two = 1.0 / (2.0 / sigma_one - sigma_one)
sigma_three = 1.0 / (2.0 / sigma_one - sigma_two)
rashba = 0.3

ALPHA1 = sigma_one / e_half
ALPHA2 = 2.0 * sigma_two / e_half
BETA2 = -sigma_one * sigma_two
ALPHA3 = 2.0 * sigma_three / e_half
BETA3 = -sigma_two * sigma_three
RH = 0.5 * rashba
NBC = -0.5 / RH


def _make_kernel(planes, chunk, aliased):
    rows_n = chunk // 8

    def kernel(valid_ref, mask_ref, f_ref, lo_ref, cur_ref, hi_ref, *rest):
        if aliased:
            out_ref, y1_ref, y2_ref = rest[1:]
        else:
            out_ref, y1_ref, y2_ref = rest

        def band(q, k, rows):
            if q < 0:
                return lo_ref[k, q + HALO, rows, :]
            if q < planes:
                return cur_ref[k, q, rows, :]
            return hi_ref[k, q - planes, rows, :]

        def from_y1(q, k, rows):
            return y1_ref[k, q + 2, rows, :]

        def from_y2(q, k, rows):
            return y2_ref[k, q + 1, rows, :]

        def apply(src, q, rows):
            d_up = f_ref[0, q + 2]
            d_dn = f_ref[1, q + 2]
            bx = f_ref[2, q + 2]
            by = f_ref[3, q + 2]
            m_zn = mask_ref[0]
            m_zp = mask_ref[1]
            m_yn = mask_ref[2, :, CELLS - 128 :]
            m_yp = mask_ref[3, :, :128]
            o = [None] * 4

            def add(i, v):
                o[i] = v if o[i] is None else o[i] + v

            for k in range(4):
                m = src(q, k, rows)
                xn = src(q + 1, k, rows)
                xp = src(q - 1, k, rows)
                r = pltpu.roll(m, CELLS - DZ, 1)
                yn = jnp.concatenate([r[:, : CELLS - 128], r[:, CELLS - 128 :] * m_yn], axis=1)
                r = pltpu.roll(m, DZ, 1)
                yp = jnp.concatenate([r[:, :128] * m_yp, r[:, 128:]], axis=1)
                zn = pltpu.roll(m, CELLS - 1, 1) * m_zn
                zp = pltpu.roll(m, 1, 1) * m_zp
                nb = (xn + xp) + (yn + yp) + (zn + zp)
                dx = xn - xp
                dy = yn - yp
                if k == 0:
                    add(0, d_up * m + NBC * nb)
                    add(2, bx * m - dx)
                    add(3, by * m - dy)
                elif k == 1:
                    add(1, d_up * m + NBC * nb)
                    add(2, dy - by * m)
                    add(3, bx * m - dx)
                elif k == 2:
                    add(2, d_dn * m + NBC * nb)
                    add(0, bx * m + dx)
                    add(1, -(by * m) - dy)
                else:
                    add(3, d_dn * m + NBC * nb)
                    add(0, by * m + dy)
                    add(1, bx * m + dx)
            return o

        def run_stage(src, dst, prev, q_lo, q_hi, alpha, beta):
            for q in range(q_lo, q_hi):
                halo_plane = q < 0 or q >= planes

                def body(r, carry, q=q, halo_plane=halo_plane):
                    rows = pl.ds(pl.multiple_of(r * 8, 8), 8)
                    o = apply(src, q, rows)
                    scale = valid_ref[q + HALO] if halo_plane else None
                    for k in range(4):
                        res = (alpha * RH) * o[k]
                        if prev is not None:
                            res = res + beta * prev(q, k, rows)
                        if scale is not None:
                            res = res * scale
                        dst(q, k, rows, res)
                    return carry

                lax.fori_loop(0, rows_n, body, 0)

        def put_y1(q, k, rows, v):
            y1_ref[k, q + 2, rows, :] = v

        def put_y2(q, k, rows, v):
            y2_ref[k, q + 1, rows, :] = v

        def put_out(q, k, rows, v):
            out_ref[k, q, rows, :] = v

        run_stage(band, put_y1, None, -2, planes + 2, ALPHA1, 0.0)
        run_stage(from_y1, put_y2, band, -1, planes + 1, ALPHA2, BETA2)
        run_stage(from_y2, put_out, from_y1, 0, planes, ALPHA3, BETA3)

    return kernel


def _filter_chunk(valid, masks, fext, lo, cur_full, hi, acc, c, planes, chunk):
    aliased = acc is not None
    nb_full = cur_full.shape[2]
    blk = (4, HALO, chunk, CELLS)
    in_specs = [
        pl.BlockSpec(memory_space=pltpu.SMEM),
        pl.BlockSpec(masks.shape, lambda i: (0, 0, 0)),
        pl.BlockSpec(fext.shape, lambda i: (0, 0, 0, 0)),
        pl.BlockSpec(blk, lambda i: (0, 0, 0, 0)),
        pl.BlockSpec((4, planes, chunk, CELLS), lambda i: (0, 0, c, 0)),
        pl.BlockSpec(blk, lambda i: (0, 0, 0, 0)),
    ]
    args = [valid, masks, fext, lo, cur_full, hi]
    extra = {}
    if aliased:
        in_specs.append(pl.BlockSpec(memory_space=pl.ANY))
        args.append(acc)
        extra["input_output_aliases"] = {6: 0}
    return pl.pallas_call(
        _make_kernel(planes, chunk, aliased),
        grid=(1,),
        in_specs=in_specs,
        out_specs=pl.BlockSpec((4, planes, chunk, CELLS), lambda i: (0, 0, c, 0)),
        out_shape=jax.ShapeDtypeStruct((4, planes, nb_full, CELLS), jnp.float32),
        scratch_shapes=[
            pltpu.VMEM((4, planes + 4, chunk, CELLS), jnp.float32),
            pltpu.VMEM((4, planes + 2, chunk, CELLS), jnp.float32),
        ],
        compiler_params=pltpu.CompilerParams(vmem_limit_bytes=48 * 1024 * 1024),
        **extra,
    )(*args)


def _shift(x, axis, step):
    count = lax.axis_size(axis)
    if step > 0:
        pairs = [(i, i + 1) for i in range(count - 1)]
    else:
        pairs = [(i + 1, i) for i in range(count - 1)]
    return lax.ppermute(x, axis, pairs)


def _fields(potential, domain_blocks, block_slots, domain_offsets, held):
    ndom = lax.axis_size("dom")
    per_dev = potential.shape[2]
    d = lax.axis_index("dom")
    pot = jnp.concatenate(
        [_shift(potential[:, -2:], "grid", 1), potential, _shift(potential[:, :2], "grid", -1)], axis=1
    )
    planes = pot.shape[1]
    slot_of = block_slots[domain_blocks]
    owner = slot_of // per_dev
    locs = jnp.sum(jnp.where(owner == d, slot_of % per_dev, 0), axis=1)
    sends = jnp.moveaxis(jnp.take(pot, locs, axis=2), 2, 0)
    sends, held = lax.optimization_barrier((sends, held))
    allr = lax.all_to_all(sends, "dom", 0, 0, tiled=True)
    blocks = jnp.take(allr, lax.dynamic_index_in_dim(owner, d, 0, keepdims=False), axis=0)
    window = jnp.transpose(blocks, (1, 2, 0, 3)).reshape(4, planes, OVL * pot.shape[3])
    f = lax.dynamic_slice_in_dim(window, domain_offsets[d] * DZ, CELLS, 2)
    v, bx, by, bz = f[0], f[1], f[2], f[3]
    return jnp.stack([v + bz + (3.0 - centre), v - bz + (3.0 - centre), bx, by]), held


def per_device(bands, potential, domain_blocks, block_slots, domain_offsets):
    b = jnp.transpose(bands[0], (0, 2, 1, 3))
    planes = b.shape[1]
    nbands = b.shape[2]
    g = lax.axis_index("grid")
    ng = lax.axis_size("grid")
    chunk = CHUNK

    fext, b = _fields(potential, domain_blocks, block_slots, domain_offsets, b)

    los, his = [], []
    for c in range(nbands // chunk):
        bc = b[:, :, c * chunk : (c + 1) * chunk]
        los.append(_shift(bc[:, planes - HALO :], "grid", 1))
        his.append(_shift(bc[:, :HALO], "grid", -1))

    q = jnp.arange(-HALO, planes + HALO)
    glob = g * planes + q
    valid = ((glob >= 0) & (glob < ng * planes)).astype(jnp.float32)

    cell = jnp.arange(CELLS)
    masks = jnp.stack(
        [cell % DZ != DZ - 1, cell % DZ != 0, cell < CELLS - DZ, cell >= DZ]
    ).astype(jnp.float32)
    masks = jnp.broadcast_to(masks[:, None, :], (4, 8, CELLS))
    fext = jnp.broadcast_to(fext[:, :, None, :] / RH, fext.shape[:2] + (8, CELLS))

    acc = None
    for c in range(nbands // chunk):
        acc = _filter_chunk(valid, masks, fext, los[c], b, his[c], acc, c, planes, chunk)
    return jnp.transpose(acc, (0, 2, 1, 3))[None]


def solution(mesh):
    placed = (P("dom", None, None, "grid", None), P(None, "grid", "dom", None), P(), P(), P())
    return jax.shard_map(
        per_device,
        mesh=mesh,
        in_specs=placed,
        out_specs=P("dom", None, None, "grid", None),
        check_vma=False,
    )
```

```python
import jax
import jax.numpy as jnp
from jax import lax
from jax.experimental import pallas as pl
from jax.experimental.pallas import tpu as pltpu
from jax.sharding import PartitionSpec as P

DZ = 64
OVL = 6
CELLS = 1280
HALO = 3
CHUNK = 16


e_half = 4.5
centre = 5.0
sigma_one = e_half / (-3.5 - centre)
sigma_two = 1.0 / (2.0 / sigma_one - sigma_one)
sigma_three = 1.0 / (2.0 / sigma_one - sigma_two)
rashba = 0.3

ALPHA1 = sigma_one / e_half
ALPHA2 = 2.0 * sigma_two / e_half
BETA2 = -sigma_one * sigma_two
ALPHA3 = 2.0 * sigma_three / e_half
BETA3 = -sigma_two * sigma_three
RH = 0.5 * rashba


def _make_kernel(planes, chunk, aliased):
    rows_n = chunk // 8

    def kernel(valid_ref, f_ref, lo_ref, cur_ref, hi_ref, *rest):
        if aliased:
            out_ref, y1_ref, y2_ref = rest[1:]
        else:
            out_ref, y1_ref, y2_ref = rest
        cell = lax.broadcasted_iota(jnp.int32, (8, CELLS), 1)
        zc = cell % DZ
        m_yn = cell < CELLS - DZ
        m_yp = cell >= DZ
        m_zn = zc != DZ - 1
        m_zp = zc != 0

        def band(q, k, rows):
            if q < 0:
                return lo_ref[k, q + HALO, rows, :]
            if q < planes:
                return cur_ref[k, q, rows, :]
            return hi_ref[k, q - planes, rows, :]

        def from_y1(q, k, rows):
            return y1_ref[k, q + 2, rows, :]

        def from_y2(q, k, rows):
            return y2_ref[k, q + 1, rows, :]

        def apply(src, q, rows):
            d_up = f_ref[0, q + 2 : q + 3, :]
            d_dn = f_ref[1, q + 2 : q + 3, :]
            bx = f_ref[2, q + 2 : q + 3, :]
            by = f_ref[3, q + 2 : q + 3, :]
            o = [None] * 4

            def add(i, v):
                o[i] = v if o[i] is None else o[i] + v

            for k in range(4):
                m = src(q, k, rows)
                xn = src(q + 1, k, rows)
                xp = src(q - 1, k, rows)
                yn = jnp.where(m_yn, pltpu.roll(m, CELLS - DZ, 1), 0.0)
                yp = jnp.where(m_yp, pltpu.roll(m, DZ, 1), 0.0)
                zn = jnp.where(m_zn, pltpu.roll(m, CELLS - 1, 1), 0.0)
                zp = jnp.where(m_zp, pltpu.roll(m, 1, 1), 0.0)
                nb = (xn + xp) + (yn + yp) + (zn + zp)
                dx = RH * (xn - xp)
                dy = RH * (yn - yp)
                if k == 0:
                    add(0, d_up * m - 0.5 * nb)
                    add(2, bx * m - dx)
                    add(3, by * m - dy)
                elif k == 1:
                    add(1, d_up * m - 0.5 * nb)
                    add(2, dy - by * m)
                    add(3, bx * m - dx)
                elif k == 2:
                    add(2, d_dn * m - 0.5 * nb)
                    add(0, bx * m + dx)
                    add(1, -(by * m) - dy)
                else:
                    add(3, d_dn * m - 0.5 * nb)
                    add(0, by * m + dy)
                    add(1, bx * m + dx)
            return o

        def run_stage(src, dst, prev, q_lo, q_hi, alpha, beta):
            for q in range(q_lo, q_hi):
                halo_plane = q < 0 or q >= planes

                def body(r, carry, q=q, halo_plane=halo_plane):
                    rows = pl.ds(pl.multiple_of(r * 8, 8), 8)
                    o = apply(src, q, rows)
                    scale = valid_ref[q + HALO] if halo_plane else None
                    for k in range(4):
                        res = alpha * o[k]
                        if prev is not None:
                            res = res + beta * prev(q, k, rows)
                        if scale is not None:
                            res = res * scale
                        dst(q, k, rows, res)
                    return carry

                lax.fori_loop(0, rows_n, body, 0)

        def put_y1(q, k, rows, v):
            y1_ref[k, q + 2, rows, :] = v

        def put_y2(q, k, rows, v):
            y2_ref[k, q + 1, rows, :] = v

        def put_out(q, k, rows, v):
            out_ref[k, q, rows, :] = v

        run_stage(band, put_y1, None, -2, planes + 2, ALPHA1, 0.0)
        run_stage(from_y1, put_y2, band, -1, planes + 1, ALPHA2, BETA2)
        run_stage(from_y2, put_out, from_y1, 0, planes, ALPHA3, BETA3)

    return kernel


def _filter_chunk(valid, fext, lo, cur_full, hi, acc, c, planes, chunk):
    aliased = acc is not None
    nb_full = cur_full.shape[2]
    blk = (4, HALO, chunk, CELLS)
    in_specs = [
        pl.BlockSpec(memory_space=pltpu.SMEM),
        pl.BlockSpec(fext.shape, lambda i: (0, 0, 0)),
        pl.BlockSpec(blk, lambda i: (0, 0, 0, 0)),
        pl.BlockSpec((4, planes, chunk, CELLS), lambda i: (0, 0, c, 0)),
        pl.BlockSpec(blk, lambda i: (0, 0, 0, 0)),
    ]
    args = [valid, fext, lo, cur_full, hi]
    extra = {}
    if aliased:
        in_specs.append(pl.BlockSpec(memory_space=pl.ANY))
        args.append(acc)
        extra["input_output_aliases"] = {5: 0}
    return pl.pallas_call(
        _make_kernel(planes, chunk, aliased),
        grid=(1,),
        in_specs=in_specs,
        out_specs=pl.BlockSpec((4, planes, chunk, CELLS), lambda i: (0, 0, c, 0)),
        out_shape=jax.ShapeDtypeStruct((4, planes, nb_full, CELLS), jnp.float32),
        scratch_shapes=[
            pltpu.VMEM((4, planes + 4, chunk, CELLS), jnp.float32),
            pltpu.VMEM((4, planes + 2, chunk, CELLS), jnp.float32),
        ],
        compiler_params=pltpu.CompilerParams(vmem_limit_bytes=48 * 1024 * 1024),
        **extra,
    )(*args)


def _shift(x, axis, step):
    count = lax.axis_size(axis)
    if step > 0:
        pairs = [(i, i + 1) for i in range(count - 1)]
    else:
        pairs = [(i + 1, i) for i in range(count - 1)]
    return lax.ppermute(x, axis, pairs)


def _fields(potential, domain_blocks, block_slots, domain_offsets, held):
    ndom = lax.axis_size("dom")
    per_dev = potential.shape[2]
    d = lax.axis_index("dom")
    pot = jnp.concatenate(
        [_shift(potential[:, -2:], "grid", 1), potential, _shift(potential[:, :2], "grid", -1)], axis=1
    )
    planes = pot.shape[1]
    slot_of = block_slots[domain_blocks]
    owner = slot_of // per_dev
    locs = jnp.sum(jnp.where(owner == d, slot_of % per_dev, 0), axis=1)
    sends = jnp.moveaxis(jnp.take(pot, locs, axis=2), 2, 0)
    sends, held = lax.optimization_barrier((sends, held))
    allr = lax.all_to_all(sends, "dom", 0, 0, tiled=True)
    blocks = jnp.take(allr, lax.dynamic_index_in_dim(owner, d, 0, keepdims=False), axis=0)
    window = jnp.transpose(blocks, (1, 2, 0, 3)).reshape(4, planes, OVL * pot.shape[3])
    f = lax.dynamic_slice_in_dim(window, domain_offsets[d] * DZ, CELLS, 2)
    v, bx, by, bz = f[0], f[1], f[2], f[3]
    return jnp.stack([v + bz + (3.0 - centre), v - bz + (3.0 - centre), bx, by]), held


def per_device(bands, potential, domain_blocks, block_slots, domain_offsets):
    b = jnp.transpose(bands[0], (0, 2, 1, 3))
    planes = b.shape[1]
    nbands = b.shape[2]
    g = lax.axis_index("grid")
    ng = lax.axis_size("grid")
    chunk = CHUNK

    fext, b = _fields(potential, domain_blocks, block_slots, domain_offsets, b)

    def send(c, src):
        bc = src[:, :, c * chunk : (c + 1) * chunk]
        return _shift(bc[:, planes - HALO :], "grid", 1), _shift(bc[:, :HALO], "grid", -1)

    nch = nbands // chunk
    lead = 2
    halos = [send(c, b) if c < lead else None for c in range(nch)]

    q = jnp.arange(-HALO, planes + HALO)
    glob = g * planes + q
    valid = ((glob >= 0) & (glob < ng * planes)).astype(jnp.float32)

    acc = None
    for c in range(nch):
        lo, hi = halos[c]
        acc = _filter_chunk(valid, fext, lo, b, hi, acc, c, planes, chunk)
        if c + lead < nch:
            later, acc = lax.optimization_barrier((b, acc))
            halos[c + lead] = send(c + lead, later)
    return jnp.transpose(acc, (0, 2, 1, 3))[None]


def solution(mesh):
    placed = (P("dom", None, None, "grid", None), P(None, "grid", "dom", None), P(), P(), P())
    return jax.shard_map(
        per_device,
        mesh=mesh,
        in_specs=placed,
        out_specs=P("dom", None, None, "grid", None),
        check_vma=False,
    )
```

```python
import jax
import jax.numpy as jnp
from jax import lax
from jax.experimental import pallas as pl
from jax.experimental.pallas import tpu as pltpu
from jax.sharding import PartitionSpec as P

DZ = 64
OVL = 6
CELLS = 1280
HALO = 3
CHUNK = 16


e_half = 4.5
centre = 5.0
sigma_one = e_half / (-3.5 - centre)
sigma_two = 1.0 / (2.0 / sigma_one - sigma_one)
sigma_three = 1.0 / (2.0 / sigma_one - sigma_two)
rashba = 0.3

ALPHA1 = sigma_one / e_half
ALPHA2 = 2.0 * sigma_two / e_half
BETA2 = -sigma_one * sigma_two
ALPHA3 = 2.0 * sigma_three / e_half
BETA3 = -sigma_two * sigma_three
RH = 0.5 * rashba


def _make_kernel(planes, chunk, aliased):
    rows_n = chunk // 8

    def kernel(valid_ref, f_ref, lo_ref, cur_ref, hi_ref, *rest):
        if aliased:
            out_ref, y1_ref, y2_ref = rest[1:]
        else:
            out_ref, y1_ref, y2_ref = rest
        cell = lax.broadcasted_iota(jnp.int32, (8, CELLS), 1)
        zc = cell % DZ
        m_yn = cell < CELLS - DZ
        m_yp = cell >= DZ
        m_zn = zc != DZ - 1
        m_zp = zc != 0

        def band(q, k, rows):
            if q < 0:
                return lo_ref[k, q + HALO, rows, :]
            if q < planes:
                return cur_ref[k, q, rows, :]
            return hi_ref[k, q - planes, rows, :]

        def from_y1(q, k, rows):
            return y1_ref[k, q + 2, rows, :]

        def from_y2(q, k, rows):
            return y2_ref[k, q + 1, rows, :]

        def apply(src, q, rows):
            d_up = f_ref[0, q + 2 : q + 3, :]
            d_dn = f_ref[1, q + 2 : q + 3, :]
            bx = f_ref[2, q + 2 : q + 3, :]
            by = f_ref[3, q + 2 : q + 3, :]
            o = [None] * 4

            def add(i, v):
                o[i] = v if o[i] is None else o[i] + v

            for k in range(4):
                m = src(q, k, rows)
                xn = src(q + 1, k, rows)
                xp = src(q - 1, k, rows)
                yn = jnp.where(m_yn, pltpu.roll(m, CELLS - DZ, 1), 0.0)
                yp = jnp.where(m_yp, pltpu.roll(m, DZ, 1), 0.0)
                zn = jnp.where(m_zn, pltpu.roll(m, CELLS - 1, 1), 0.0)
                zp = jnp.where(m_zp, pltpu.roll(m, 1, 1), 0.0)
                nb = (xn + xp) + (yn + yp) + (zn + zp)
                dx = RH * (xn - xp)
                dy = RH * (yn - yp)
                if k == 0:
                    add(0, d_up * m - 0.5 * nb)
                    add(2, bx * m - dx)
                    add(3, by * m - dy)
                elif k == 1:
                    add(1, d_up * m - 0.5 * nb)
                    add(2, dy - by * m)
                    add(3, bx * m - dx)
                elif k == 2:
                    add(2, d_dn * m - 0.5 * nb)
                    add(0, bx * m + dx)
                    add(1, -(by * m) - dy)
                else:
                    add(3, d_dn * m - 0.5 * nb)
                    add(0, by * m + dy)
                    add(1, bx * m + dx)
            return o

        def run_stage(src, dst, prev, q_lo, q_hi, alpha, beta):
            for q in range(q_lo, q_hi):
                halo_plane = q < 0 or q >= planes

                def body(r, carry, q=q, halo_plane=halo_plane):
                    rows = pl.ds(pl.multiple_of(r * 8, 8), 8)
                    o = apply(src, q, rows)
                    scale = valid_ref[q + HALO] if halo_plane else None
                    for k in range(4):
                        res = alpha * o[k]
                        if prev is not None:
                            res = res + beta * prev(q, k, rows)
                        if scale is not None:
                            res = res * scale
                        dst(q, k, rows, res)
                    return carry

                lax.fori_loop(0, rows_n, body, 0)

        def put_y1(q, k, rows, v):
            y1_ref[k, q + 2, rows, :] = v

        def put_y2(q, k, rows, v):
            y2_ref[k, q + 1, rows, :] = v

        def put_out(q, k, rows, v):
            out_ref[k, q, rows, :] = v

        run_stage(band, put_y1, None, -2, planes + 2, ALPHA1, 0.0)
        run_stage(from_y1, put_y2, band, -1, planes + 1, ALPHA2, BETA2)
        run_stage(from_y2, put_out, from_y1, 0, planes, ALPHA3, BETA3)

    return kernel


def _filter_chunk(valid, fext, lo, cur_full, hi, acc, c, planes, chunk):
    aliased = acc is not None
    nb_full = cur_full.shape[2]
    rows = 8
    steps = chunk // rows
    base = c * steps
    blk = (4, HALO, rows, CELLS)
    in_specs = [
        pl.BlockSpec(memory_space=pltpu.SMEM),
        pl.BlockSpec(fext.shape, lambda i: (0, 0, 0)),
        pl.BlockSpec(blk, lambda i: (0, 0, i, 0)),
        pl.BlockSpec((4, planes, rows, CELLS), lambda i: (0, 0, base + i, 0)),
        pl.BlockSpec(blk, lambda i: (0, 0, i, 0)),
    ]
    args = [valid, fext, lo, cur_full, hi]
    extra = {}
    if aliased:
        in_specs.append(pl.BlockSpec(memory_space=pl.ANY))
        args.append(acc)
        extra["input_output_aliases"] = {5: 0}
    return pl.pallas_call(
        _make_kernel(planes, rows, aliased),
        grid=(steps,),
        in_specs=in_specs,
        out_specs=pl.BlockSpec((4, planes, rows, CELLS), lambda i: (0, 0, base + i, 0)),
        out_shape=jax.ShapeDtypeStruct((4, planes, nb_full, CELLS), jnp.float32),
        scratch_shapes=[
            pltpu.VMEM((4, planes + 4, rows, CELLS), jnp.float32),
            pltpu.VMEM((4, planes + 2, rows, CELLS), jnp.float32),
        ],
        compiler_params=pltpu.CompilerParams(vmem_limit_bytes=48 * 1024 * 1024),
        **extra,
    )(*args)


def _shift(x, axis, step):
    count = lax.axis_size(axis)
    if step > 0:
        pairs = [(i, i + 1) for i in range(count - 1)]
    else:
        pairs = [(i + 1, i) for i in range(count - 1)]
    return lax.ppermute(x, axis, pairs)


def _fields(potential, domain_blocks, block_slots, domain_offsets, held):
    ndom = lax.axis_size("dom")
    per_dev = potential.shape[2]
    d = lax.axis_index("dom")
    pot = jnp.concatenate(
        [_shift(potential[:, -2:], "grid", 1), potential, _shift(potential[:, :2], "grid", -1)], axis=1
    )
    planes = pot.shape[1]
    slot_of = block_slots[domain_blocks]
    owner = slot_of // per_dev
    locs = jnp.sum(jnp.where(owner == d, slot_of % per_dev, 0), axis=1)
    sends = jnp.moveaxis(jnp.take(pot, locs, axis=2), 2, 0)
    sends, held = lax.optimization_barrier((sends, held))
    allr = lax.all_to_all(sends, "dom", 0, 0, tiled=True)
    blocks = jnp.take(allr, lax.dynamic_index_in_dim(owner, d, 0, keepdims=False), axis=0)
    window = jnp.transpose(blocks, (1, 2, 0, 3)).reshape(4, planes, OVL * pot.shape[3])
    f = lax.dynamic_slice_in_dim(window, domain_offsets[d] * DZ, CELLS, 2)
    v, bx, by, bz = f[0], f[1], f[2], f[3]
    return jnp.stack([v + bz + (3.0 - centre), v - bz + (3.0 - centre), bx, by]), held


def per_device(bands, potential, domain_blocks, block_slots, domain_offsets):
    b = jnp.transpose(bands[0], (0, 2, 1, 3))
    planes = b.shape[1]
    nbands = b.shape[2]
    g = lax.axis_index("grid")
    ng = lax.axis_size("grid")
    chunk = CHUNK

    fext, b = _fields(potential, domain_blocks, block_slots, domain_offsets, b)

    los, his = [], []
    for c in range(nbands // chunk):
        bc = b[:, :, c * chunk : (c + 1) * chunk]
        los.append(_shift(bc[:, planes - HALO :], "grid", 1))
        his.append(_shift(bc[:, :HALO], "grid", -1))

    q = jnp.arange(-HALO, planes + HALO)
    glob = g * planes + q
    valid = ((glob >= 0) & (glob < ng * planes)).astype(jnp.float32)

    acc = None
    for c in range(nbands // chunk):
        acc = _filter_chunk(valid, fext, los[c], b, his[c], acc, c, planes, chunk)
    return jnp.transpose(acc, (0, 2, 1, 3))[None]


def solution(mesh):
    placed = (P("dom", None, None, "grid", None), P(None, "grid", "dom", None), P(), P(), P())
    return jax.shard_map(
        per_device,
        mesh=mesh,
        in_specs=placed,
        out_specs=P("dom", None, None, "grid", None),
        check_vma=False,
    )
```

```python
import jax
import jax.numpy as jnp
from jax import lax
from jax.experimental import pallas as pl
from jax.experimental.pallas import tpu as pltpu
from jax.sharding import PartitionSpec as P

DZ = 64
OVL = 6
CELLS = 1280
HALO = 3
CHUNK = 64


e_half = 4.5
centre = 5.0
sigma_one = e_half / (-3.5 - centre)
sigma_two = 1.0 / (2.0 / sigma_one - sigma_one)
sigma_three = 1.0 / (2.0 / sigma_one - sigma_two)
rashba = 0.3

ALPHA1 = sigma_one / e_half
ALPHA2 = 2.0 * sigma_two / e_half
BETA2 = -sigma_one * sigma_two
ALPHA3 = 2.0 * sigma_three / e_half
BETA3 = -sigma_two * sigma_three
RH = 0.5 * rashba


def _make_kernel(planes, chunk, aliased):
    rows_n = chunk // 8

    def kernel(valid_ref, f_ref, lo_ref, cur_ref, hi_ref, *rest):
        if aliased:
            out_ref, y1_ref, y2_ref = rest[1:]
        else:
            out_ref, y1_ref, y2_ref = rest
        cell = lax.broadcasted_iota(jnp.int32, (8, CELLS), 1)
        zc = cell % DZ
        m_yn = cell < CELLS - DZ
        m_yp = cell >= DZ
        m_zn = zc != DZ - 1
        m_zp = zc != 0

        def band(q, k, rows):
            if q < 0:
                return lo_ref[k, q + HALO, rows, :]
            if q < planes:
                return cur_ref[k, q, rows, :]
            return hi_ref[k, q - planes, rows, :]

        def from_y1(q, k, rows):
            return y1_ref[k, q + 2, rows, :]

        def from_y2(q, k, rows):
            return y2_ref[k, q + 1, rows, :]

        def apply(src, q, rows):
            d_up = f_ref[0, q + 2 : q + 3, :]
            d_dn = f_ref[1, q + 2 : q + 3, :]
            bx = f_ref[2, q + 2 : q + 3, :]
            by = f_ref[3, q + 2 : q + 3, :]
            o = [None] * 4

            def add(i, v):
                o[i] = v if o[i] is None else o[i] + v

            for k in range(4):
                m = src(q, k, rows)
                xn = src(q + 1, k, rows)
                xp = src(q - 1, k, rows)
                yn = jnp.where(m_yn, pltpu.roll(m, CELLS - DZ, 1), 0.0)
                yp = jnp.where(m_yp, pltpu.roll(m, DZ, 1), 0.0)
                zn = jnp.where(m_zn, pltpu.roll(m, CELLS - 1, 1), 0.0)
                zp = jnp.where(m_zp, pltpu.roll(m, 1, 1), 0.0)
                nb = (xn + xp) + (yn + yp) + (zn + zp)
                dx = RH * (xn - xp)
                dy = RH * (yn - yp)
                if k == 0:
                    add(0, d_up * m - 0.5 * nb)
                    add(2, bx * m - dx)
                    add(3, by * m - dy)
                elif k == 1:
                    add(1, d_up * m - 0.5 * nb)
                    add(2, dy - by * m)
                    add(3, bx * m - dx)
                elif k == 2:
                    add(2, d_dn * m - 0.5 * nb)
                    add(0, bx * m + dx)
                    add(1, -(by * m) - dy)
                else:
                    add(3, d_dn * m - 0.5 * nb)
                    add(0, by * m + dy)
                    add(1, bx * m + dx)
            return o

        def run_stage(src, dst, prev, q_lo, q_hi, alpha, beta):
            for q in range(q_lo, q_hi):
                halo_plane = q < 0 or q >= planes

                def body(r, carry, q=q, halo_plane=halo_plane):
                    rows = pl.ds(pl.multiple_of(r * 8, 8), 8)
                    o = apply(src, q, rows)
                    scale = valid_ref[q + HALO] if halo_plane else None
                    for k in range(4):
                        res = alpha * o[k]
                        if prev is not None:
                            res = res + beta * prev(q, k, rows)
                        if scale is not None:
                            res = res * scale
                        dst(q, k, rows, res)
                    return carry

                lax.fori_loop(0, rows_n, body, 0)

        def put_y1(q, k, rows, v):
            y1_ref[k, q + 2, rows, :] = v

        def put_y2(q, k, rows, v):
            y2_ref[k, q + 1, rows, :] = v

        def put_out(q, k, rows, v):
            out_ref[k, q, rows, :] = v

        run_stage(band, put_y1, None, -2, planes + 2, ALPHA1, 0.0)
        run_stage(from_y1, put_y2, band, -1, planes + 1, ALPHA2, BETA2)
        run_stage(from_y2, put_out, from_y1, 0, planes, ALPHA3, BETA3)

    return kernel


def _filter_chunk(valid, fext, lo, cur_full, hi, acc, c, planes, chunk):
    aliased = acc is not None
    nb_full = cur_full.shape[2]
    rows = 8
    steps = chunk // rows
    base = c * steps
    blk = (4, HALO, rows, CELLS)
    in_specs = [
        pl.BlockSpec(memory_space=pltpu.SMEM),
        pl.BlockSpec(fext.shape, lambda i: (0, 0, 0)),
        pl.BlockSpec(blk, lambda i: (0, 0, i, 0)),
        pl.BlockSpec((4, planes, rows, CELLS), lambda i: (0, 0, base + i, 0)),
        pl.BlockSpec(blk, lambda i: (0, 0, i, 0)),
    ]
    args = [valid, fext, lo, cur_full, hi]
    extra = {}
    if aliased:
        in_specs.append(pl.BlockSpec(memory_space=pl.ANY))
        args.append(acc)
        extra["input_output_aliases"] = {5: 0}
    return pl.pallas_call(
        _make_kernel(planes, rows, aliased),
        grid=(steps,),
        in_specs=in_specs,
        out_specs=pl.BlockSpec((4, planes, rows, CELLS), lambda i: (0, 0, base + i, 0)),
        out_shape=jax.ShapeDtypeStruct((4, planes, nb_full, CELLS), jnp.float32),
        scratch_shapes=[
            pltpu.VMEM((4, planes + 4, rows, CELLS), jnp.float32),
            pltpu.VMEM((4, planes + 2, rows, CELLS), jnp.float32),
        ],
        compiler_params=pltpu.CompilerParams(vmem_limit_bytes=48 * 1024 * 1024),
        **extra,
    )(*args)


def _shift(x, axis, step):
    count = lax.axis_size(axis)
    if step > 0:
        pairs = [(i, i + 1) for i in range(count - 1)]
    else:
        pairs = [(i + 1, i) for i in range(count - 1)]
    return lax.ppermute(x, axis, pairs)


def _fields(potential, domain_blocks, block_slots, domain_offsets, held):
    ndom = lax.axis_size("dom")
    per_dev = potential.shape[2]
    d = lax.axis_index("dom")
    pot = jnp.concatenate(
        [_shift(potential[:, -2:], "grid", 1), potential, _shift(potential[:, :2], "grid", -1)], axis=1
    )
    planes = pot.shape[1]
    slot_of = block_slots[domain_blocks]
    owner = slot_of // per_dev
    locs = jnp.sum(jnp.where(owner == d, slot_of % per_dev, 0), axis=1)
    sends = jnp.moveaxis(jnp.take(pot, locs, axis=2), 2, 0)
    sends, held = lax.optimization_barrier((sends, held))
    allr = lax.all_to_all(sends, "dom", 0, 0, tiled=True)
    blocks = jnp.take(allr, lax.dynamic_index_in_dim(owner, d, 0, keepdims=False), axis=0)
    window = jnp.transpose(blocks, (1, 2, 0, 3)).reshape(4, planes, OVL * pot.shape[3])
    f = lax.dynamic_slice_in_dim(window, domain_offsets[d] * DZ, CELLS, 2)
    v, bx, by, bz = f[0], f[1], f[2], f[3]
    return jnp.stack([v + bz + (3.0 - centre), v - bz + (3.0 - centre), bx, by]), held


def per_device(bands, potential, domain_blocks, block_slots, domain_offsets):
    b = jnp.transpose(bands[0], (0, 2, 1, 3))
    planes = b.shape[1]
    nbands = b.shape[2]
    g = lax.axis_index("grid")
    ng = lax.axis_size("grid")
    chunk = CHUNK

    fext, b = _fields(potential, domain_blocks, block_slots, domain_offsets, b)

    los, his = [], []
    for c in range(nbands // chunk):
        bc = b[:, :, c * chunk : (c + 1) * chunk]
        los.append(_shift(bc[:, planes - HALO :], "grid", 1))
        his.append(_shift(bc[:, :HALO], "grid", -1))

    q = jnp.arange(-HALO, planes + HALO)
    glob = g * planes + q
    valid = ((glob >= 0) & (glob < ng * planes)).astype(jnp.float32)

    acc = None
    for c in range(nbands // chunk):
        acc = _filter_chunk(valid, fext, los[c], b, his[c], acc, c, planes, chunk)
    return jnp.transpose(acc, (0, 2, 1, 3))[None]


def solution(mesh):
    placed = (P("dom", None, None, "grid", None), P(None, "grid", "dom", None), P(), P(), P())
    return jax.shard_map(
        per_device,
        mesh=mesh,
        in_specs=placed,
        out_specs=P("dom", None, None, "grid", None),
        check_vma=False,
    )
```

```python
import jax
import jax.numpy as jnp
from jax import lax
from jax.experimental import pallas as pl
from jax.experimental.pallas import tpu as pltpu
from jax.sharding import PartitionSpec as P

DZ = 64
OVL = 6
CELLS = 1280
HALO = 3
CHUNK = 32


e_half = 4.5
centre = 5.0
sigma_one = e_half / (-3.5 - centre)
sigma_two = 1.0 / (2.0 / sigma_one - sigma_one)
sigma_three = 1.0 / (2.0 / sigma_one - sigma_two)
rashba = 0.3

ALPHA1 = sigma_one / e_half
ALPHA2 = 2.0 * sigma_two / e_half
BETA2 = -sigma_one * sigma_two
ALPHA3 = 2.0 * sigma_three / e_half
BETA3 = -sigma_two * sigma_three
RH = 0.5 * rashba


def _make_kernel(planes, chunk, aliased):
    rows_n = chunk // 8

    def kernel(valid_ref, f_ref, lo_ref, cur_ref, hi_ref, *rest):
        if aliased:
            out_ref, y1_ref, y2_ref = rest[1:]
        else:
            out_ref, y1_ref, y2_ref = rest
        cell = lax.broadcasted_iota(jnp.int32, (8, CELLS), 1)
        zc = cell % DZ
        m_yn = cell < CELLS - DZ
        m_yp = cell >= DZ
        m_zn = zc != DZ - 1
        m_zp = zc != 0

        def band(q, k, rows):
            if q < 0:
                return lo_ref[k, q + HALO, rows, :]
            if q < planes:
                return cur_ref[k, q, rows, :]
            return hi_ref[k, q - planes, rows, :]

        def from_y1(q, k, rows):
            return y1_ref[k, q + 2, rows, :]

        def from_y2(q, k, rows):
            return y2_ref[k, q + 1, rows, :]

        def apply(src, q, rows):
            d_up = f_ref[0, q + 2 : q + 3, :]
            d_dn = f_ref[1, q + 2 : q + 3, :]
            bx = f_ref[2, q + 2 : q + 3, :]
            by = f_ref[3, q + 2 : q + 3, :]
            o = [None] * 4

            def add(i, v):
                o[i] = v if o[i] is None else o[i] + v

            for k in range(4):
                m = src(q, k, rows)
                xn = src(q + 1, k, rows)
                xp = src(q - 1, k, rows)
                yn = jnp.where(m_yn, pltpu.roll(m, CELLS - DZ, 1), 0.0)
                yp = jnp.where(m_yp, pltpu.roll(m, DZ, 1), 0.0)
                zn = jnp.where(m_zn, pltpu.roll(m, CELLS - 1, 1), 0.0)
                zp = jnp.where(m_zp, pltpu.roll(m, 1, 1), 0.0)
                nb = (xn + xp) + (yn + yp) + (zn + zp)
                dx = RH * (xn - xp)
                dy = RH * (yn - yp)
                if k == 0:
                    add(0, d_up * m - 0.5 * nb)
                    add(2, bx * m - dx)
                    add(3, by * m - dy)
                elif k == 1:
                    add(1, d_up * m - 0.5 * nb)
                    add(2, dy - by * m)
                    add(3, bx * m - dx)
                elif k == 2:
                    add(2, d_dn * m - 0.5 * nb)
                    add(0, bx * m + dx)
                    add(1, -(by * m) - dy)
                else:
                    add(3, d_dn * m - 0.5 * nb)
                    add(0, by * m + dy)
                    add(1, bx * m + dx)
            return o

        def run_stage(src, dst, prev, q_lo, q_hi, alpha, beta):
            for q in range(q_lo, q_hi):
                halo_plane = q < 0 or q >= planes

                def body(r, carry, q=q, halo_plane=halo_plane):
                    rows = pl.ds(pl.multiple_of(r * 8, 8), 8)
                    o = apply(src, q, rows)
                    scale = valid_ref[q + HALO] if halo_plane else None
                    for k in range(4):
                        res = alpha * o[k]
                        if prev is not None:
                            res = res + beta * prev(q, k, rows)
                        if scale is not None:
                            res = res * scale
                        dst(q, k, rows, res)
                    return carry

                lax.fori_loop(0, rows_n, body, 0)

        def put_y1(q, k, rows, v):
            y1_ref[k, q + 2, rows, :] = v

        def put_y2(q, k, rows, v):
            y2_ref[k, q + 1, rows, :] = v

        def put_out(q, k, rows, v):
            out_ref[k, q, rows, :] = v

        run_stage(band, put_y1, None, -2, planes + 2, ALPHA1, 0.0)
        run_stage(from_y1, put_y2, band, -1, planes + 1, ALPHA2, BETA2)
        run_stage(from_y2, put_out, from_y1, 0, planes, ALPHA3, BETA3)

    return kernel


def _filter_chunk(valid, fext, lo, cur_full, hi, acc, c, planes, chunk):
    aliased = acc is not None
    nb_full = cur_full.shape[2]
    rows = 8
    steps = chunk // rows
    base = c * steps
    blk = (4, HALO, rows, CELLS)
    in_specs = [
        pl.BlockSpec(memory_space=pltpu.SMEM),
        pl.BlockSpec(fext.shape, lambda i: (0, 0, 0)),
        pl.BlockSpec(blk, lambda i: (0, 0, i, 0)),
        pl.BlockSpec((4, planes, rows, CELLS), lambda i: (0, 0, base + i, 0)),
        pl.BlockSpec(blk, lambda i: (0, 0, i, 0)),
    ]
    args = [valid, fext, lo, cur_full, hi]
    extra = {}
    if aliased:
        in_specs.append(pl.BlockSpec(memory_space=pl.ANY))
        args.append(acc)
        extra["input_output_aliases"] = {5: 0}
    return pl.pallas_call(
        _make_kernel(planes, rows, aliased),
        grid=(steps,),
        in_specs=in_specs,
        out_specs=pl.BlockSpec((4, planes, rows, CELLS), lambda i: (0, 0, base + i, 0)),
        out_shape=jax.ShapeDtypeStruct((4, planes, nb_full, CELLS), jnp.float32),
        scratch_shapes=[
            pltpu.VMEM((4, planes + 4, rows, CELLS), jnp.float32),
            pltpu.VMEM((4, planes + 2, rows, CELLS), jnp.float32),
        ],
        compiler_params=pltpu.CompilerParams(vmem_limit_bytes=48 * 1024 * 1024),
        **extra,
    )(*args)


def _shift(x, axis, step):
    count = lax.axis_size(axis)
    if step > 0:
        pairs = [(i, i + 1) for i in range(count - 1)]
    else:
        pairs = [(i + 1, i) for i in range(count - 1)]
    return lax.ppermute(x, axis, pairs)


def _fields(potential, domain_blocks, block_slots, domain_offsets, held):
    ndom = lax.axis_size("dom")
    per_dev = potential.shape[2]
    d = lax.axis_index("dom")
    pot = jnp.concatenate(
        [_shift(potential[:, -2:], "grid", 1), potential, _shift(potential[:, :2], "grid", -1)], axis=1
    )
    planes = pot.shape[1]
    slot_of = block_slots[domain_blocks]
    owner = slot_of // per_dev
    locs = jnp.sum(jnp.where(owner == d, slot_of % per_dev, 0), axis=1)
    sends = jnp.moveaxis(jnp.take(pot, locs, axis=2), 2, 0)
    allr = lax.all_to_all(sends, "dom", 0, 0, tiled=True)
    allr, held = lax.optimization_barrier((allr, held))
    blocks = jnp.take(allr, lax.dynamic_index_in_dim(owner, d, 0, keepdims=False), axis=0)
    window = jnp.transpose(blocks, (1, 2, 0, 3)).reshape(4, planes, OVL * pot.shape[3])
    f = lax.dynamic_slice_in_dim(window, domain_offsets[d] * DZ, CELLS, 2)
    v, bx, by, bz = f[0], f[1], f[2], f[3]
    return jnp.stack([v + bz + (3.0 - centre), v - bz + (3.0 - centre), bx, by]), held


def per_device(bands, potential, domain_blocks, block_slots, domain_offsets):
    b = jnp.transpose(bands[0], (0, 2, 1, 3))
    planes = b.shape[1]
    nbands = b.shape[2]
    g = lax.axis_index("grid")
    ng = lax.axis_size("grid")
    chunk = CHUNK

    fext, b = _fields(potential, domain_blocks, block_slots, domain_offsets, b)

    los, his = [], []
    for c in range(nbands // chunk):
        bc = b[:, :, c * chunk : (c + 1) * chunk]
        los.append(_shift(bc[:, planes - HALO :], "grid", 1))
        his.append(_shift(bc[:, :HALO], "grid", -1))

    q = jnp.arange(-HALO, planes + HALO)
    glob = g * planes + q
    valid = ((glob >= 0) & (glob < ng * planes)).astype(jnp.float32)

    acc = None
    for c in range(nbands // chunk):
        acc = _filter_chunk(valid, fext, los[c], b, his[c], acc, c, planes, chunk)
    return jnp.transpose(acc, (0, 2, 1, 3))[None]


def solution(mesh):
    placed = (P("dom", None, None, "grid", None), P(None, "grid", "dom", None), P(), P(), P())
    return jax.shard_map(
        per_device,
        mesh=mesh,
        in_specs=placed,
        out_specs=P("dom", None, None, "grid", None),
        check_vma=False,
    )
```

```python
import jax
import jax.numpy as jnp
from jax import lax
from jax.experimental import pallas as pl
from jax.experimental.pallas import tpu as pltpu
from jax.sharding import PartitionSpec as P


DZ = 64
OVL = 6
CELLS = 1280
HALO = 3
CHUNK = 32


e_half = 4.5
centre = 5.0
sigma_one = e_half / (-3.5 - centre)
sigma_two = 1.0 / (2.0 / sigma_one - sigma_one)
sigma_three = 1.0 / (2.0 / sigma_one - sigma_two)
rashba = 0.3

ALPHA1 = sigma_one / e_half
ALPHA2 = 2.0 * sigma_two / e_half
BETA2 = -sigma_one * sigma_two
ALPHA3 = 2.0 * sigma_three / e_half
BETA3 = -sigma_two * sigma_three
RH = 0.5 * rashba


def _make_kernel(planes, chunk, aliased):
    rows_n = chunk // 8

    def kernel(valid_ref, f_ref, lo_ref, cur_ref, hi_ref, *rest):
        if aliased:
            out_ref, y1_ref, y2_ref = rest[1:]
        else:
            out_ref, y1_ref, y2_ref = rest
        cell = lax.broadcasted_iota(jnp.int32, (8, CELLS), 1)
        zc = cell % DZ
        m_yn = cell < CELLS - DZ
        m_yp = cell >= DZ
        m_zn = zc != DZ - 1
        m_zp = zc != 0

        def band(q, k, rows):
            if q < 0:
                return lo_ref[k, q + HALO, rows, :]
            if q < planes:
                return cur_ref[k, q, rows, :]
            return hi_ref[k, q - planes, rows, :]

        def from_y1(q, k, rows):
            return y1_ref[k, q + 2, rows, :]

        def from_y2(q, k, rows):
            return y2_ref[k, q + 1, rows, :]

        def apply(src, q, rows):
            d_up = f_ref[0, q + 2 : q + 3, :]
            d_dn = f_ref[1, q + 2 : q + 3, :]
            bx = f_ref[2, q + 2 : q + 3, :]
            by = f_ref[3, q + 2 : q + 3, :]
            o = [None] * 4

            def add(i, v):
                o[i] = v if o[i] is None else o[i] + v

            for k in range(4):
                m = src(q, k, rows)
                xn = src(q + 1, k, rows)
                xp = src(q - 1, k, rows)
                yn = jnp.where(m_yn, pltpu.roll(m, CELLS - DZ, 1), 0.0)
                yp = jnp.where(m_yp, pltpu.roll(m, DZ, 1), 0.0)
                zn = jnp.where(m_zn, pltpu.roll(m, CELLS - 1, 1), 0.0)
                zp = jnp.where(m_zp, pltpu.roll(m, 1, 1), 0.0)
                nb = (xn + xp) + (yn + yp) + (zn + zp)
                dx = RH * (xn - xp)
                dy = RH * (yn - yp)
                if k == 0:
                    add(0, d_up * m - 0.5 * nb)
                    add(2, bx * m - dx)
                    add(3, by * m - dy)
                elif k == 1:
                    add(1, d_up * m - 0.5 * nb)
                    add(2, dy - by * m)
                    add(3, bx * m - dx)
                elif k == 2:
                    add(2, d_dn * m - 0.5 * nb)
                    add(0, bx * m + dx)
                    add(1, -(by * m) - dy)
                else:
                    add(3, d_dn * m - 0.5 * nb)
                    add(0, by * m + dy)
                    add(1, bx * m + dx)
            return o

        def run_stage(src, dst, prev, q_lo, q_hi, alpha, beta):
            for q in range(q_lo, q_hi):
                halo_plane = q < 0 or q >= planes

                def body(r, carry, q=q, halo_plane=halo_plane):
                    rows = pl.ds(pl.multiple_of(r * 8, 8), 8)
                    o = apply(src, q, rows)
                    scale = valid_ref[q + HALO] if halo_plane else None
                    for k in range(4):
                        res = alpha * o[k]
                        if prev is not None:
                            res = res + beta * prev(q, k, rows)
                        if scale is not None:
                            res = res * scale
                        dst(q, k, rows, res)
                    return carry

                lax.fori_loop(0, rows_n, body, 0)

        def put_y1(q, k, rows, v):
            y1_ref[k, q + 2, rows, :] = v

        def put_y2(q, k, rows, v):
            y2_ref[k, q + 1, rows, :] = v

        def put_out(q, k, rows, v):
            out_ref[k, q, rows, :] = v

        run_stage(band, put_y1, None, -2, planes + 2, ALPHA1, 0.0)
        run_stage(from_y1, put_y2, band, -1, planes + 1, ALPHA2, BETA2)
        run_stage(from_y2, put_out, from_y1, 0, planes, ALPHA3, BETA3)

    return kernel


def _filter_chunk(valid, fext, lo, cur_full, hi, acc, c, planes, chunk):
    aliased = acc is not None
    nb_full = cur_full.shape[2]
    rows = 8
    steps = chunk // rows
    base = c * steps
    blk = (4, HALO, rows, CELLS)
    in_specs = [
        pl.BlockSpec(memory_space=pltpu.SMEM),
        pl.BlockSpec(fext.shape, lambda i: (0, 0, 0)),
        pl.BlockSpec(blk, lambda i: (0, 0, i, 0)),
        pl.BlockSpec((4, planes, rows, CELLS), lambda i: (0, 0, base + i, 0)),
        pl.BlockSpec(blk, lambda i: (0, 0, i, 0)),
    ]
    args = [valid, fext, lo, cur_full, hi]
    extra = {}
    if aliased:
        in_specs.append(pl.BlockSpec(memory_space=pl.ANY))
        args.append(acc)
        extra["input_output_aliases"] = {5: 0}
    return pl.pallas_call(
        _make_kernel(planes, rows, aliased),
        grid=(steps,),
        in_specs=in_specs,
        out_specs=pl.BlockSpec((4, planes, rows, CELLS), lambda i: (0, 0, base + i, 0)),
        out_shape=jax.ShapeDtypeStruct((4, planes, nb_full, CELLS), jnp.float32),
        scratch_shapes=[
            pltpu.VMEM((4, planes + 4, rows, CELLS), jnp.float32),
            pltpu.VMEM((4, planes + 2, rows, CELLS), jnp.float32),
        ],
        compiler_params=pltpu.CompilerParams(vmem_limit_bytes=48 * 1024 * 1024),
        **extra,
    )(*args)


def _shift(x, axis, step):
    count = lax.axis_size(axis)
    if step > 0:
        pairs = [(i, i + 1) for i in range(count - 1)]
    else:
        pairs = [(i + 1, i) for i in range(count - 1)]
    return lax.ppermute(x, axis, pairs)


def _fields(potential, domain_blocks, block_slots, domain_offsets, held):
    per_dev = potential.shape[2]
    d = lax.axis_index("dom")
    pot = jnp.concatenate(
        [_shift(potential[:, -2:], "grid", 1), potential, _shift(potential[:, :2], "grid", -1)], axis=1
    )
    planes = pot.shape[1]
    slot_of = block_slots[domain_blocks]
    owner = slot_of // per_dev
    locs = jnp.sum(jnp.where(owner == d, slot_of % per_dev, 0), axis=1)
    sends = jnp.moveaxis(jnp.take(pot, locs, axis=2), 2, 0)
    sends, held = lax.optimization_barrier((sends, held))
    allr = lax.all_to_all(sends, "dom", 0, 0, tiled=True)
    blocks = jnp.take(allr, lax.dynamic_index_in_dim(owner, d, 0, keepdims=False), axis=0)
    window = jnp.transpose(blocks, (1, 2, 0, 3)).reshape(4, planes, OVL * pot.shape[3])
    f = lax.dynamic_slice_in_dim(window, domain_offsets[d] * DZ, CELLS, 2)
    v, bx, by, bz = f[0], f[1], f[2], f[3]
    return jnp.stack([v + bz + (3.0 - centre), v - bz + (3.0 - centre), bx, by]), held


def _per_device(bands, potential, domain_blocks, block_slots, domain_offsets):
    b = jnp.transpose(bands[0], (0, 2, 1, 3))
    planes = b.shape[1]
    nbands = b.shape[2]
    g = lax.axis_index("grid")
    ng = lax.axis_size("grid")
    chunk = CHUNK

    fext, b = _fields(potential, domain_blocks, block_slots, domain_offsets, b)

    los, his = [], []
    for c in range(nbands // chunk):
        bc = b[:, :, c * chunk : (c + 1) * chunk]
        los.append(_shift(bc[:, planes - HALO :], "grid", 1))
        his.append(_shift(bc[:, :HALO], "grid", -1))

    q = jnp.arange(-HALO, planes + HALO)
    glob = g * planes + q
    valid = ((glob >= 0) & (glob < ng * planes)).astype(jnp.float32)

    acc = None
    for c in range(nbands // chunk):
        acc = _filter_chunk(valid, fext, los[c], b, his[c], acc, c, planes, chunk)
    return jnp.transpose(acc, (0, 2, 1, 3))[None]


def solution(mesh):
    placed = (P("dom", None, None, "grid", None), P(None, "grid", "dom", None), P(), P(), P())
    return jax.shard_map(
        _per_device,
        mesh=mesh,
        in_specs=placed,
        out_specs=P("dom", None, None, "grid", None),
        check_vma=False,
    )
```

```python
import jax
import jax.numpy as jnp
from jax import lax
from jax.experimental import pallas as pl
from jax.experimental.pallas import tpu as pltpu
from jax.sharding import PartitionSpec as P

DZ = 64
OVL = 6
CELLS = 1280
HALO = 3
CHUNK = 16


e_half = 4.5
centre = 5.0
sigma_one = e_half / (-3.5 - centre)
sigma_two = 1.0 / (2.0 / sigma_one - sigma_one)
sigma_three = 1.0 / (2.0 / sigma_one - sigma_two)
rashba = 0.3

ALPHA1 = sigma_one / e_half
ALPHA2 = 2.0 * sigma_two / e_half
BETA2 = -sigma_one * sigma_two
ALPHA3 = 2.0 * sigma_three / e_half
BETA3 = -sigma_two * sigma_three
RH = 0.5 * rashba


def _make_kernel(planes, chunk, aliased):
    rows_n = chunk // 8

    def kernel(valid_ref, f_ref, lo_ref, cur_ref, hi_ref, *rest):
        if aliased:
            out_ref, y1_ref, y2_ref = rest[1:]
        else:
            out_ref, y1_ref, y2_ref = rest
        cell = lax.broadcasted_iota(jnp.int32, (8, CELLS), 1)
        zc = cell % DZ
        m_yn = cell < CELLS - DZ
        m_yp = cell >= DZ
        m_zn = zc != DZ - 1
        m_zp = zc != 0

        def band(q, k, rows):
            if q < 0:
                return lo_ref[k, q + HALO, rows, :]
            if q < planes:
                return cur_ref[k, q, rows, :]
            return hi_ref[k, q - planes, rows, :]

        def from_y1(q, k, rows):
            return y1_ref[k, q + 2, rows, :]

        def from_y2(q, k, rows):
            return y2_ref[k, q + 1, rows, :]

        def apply(src, q, rows):
            d_up = f_ref[0, q + 2 : q + 3, :]
            d_dn = f_ref[1, q + 2 : q + 3, :]
            bx = f_ref[2, q + 2 : q + 3, :]
            by = f_ref[3, q + 2 : q + 3, :]
            o = [None] * 4

            def add(i, v):
                o[i] = v if o[i] is None else o[i] + v

            for k in range(4):
                m = src(q, k, rows)
                xn = src(q + 1, k, rows)
                xp = src(q - 1, k, rows)
                yn = jnp.where(m_yn, pltpu.roll(m, CELLS - DZ, 1), 0.0)
                yp = jnp.where(m_yp, pltpu.roll(m, DZ, 1), 0.0)
                zn = jnp.where(m_zn, pltpu.roll(m, CELLS - 1, 1), 0.0)
                zp = jnp.where(m_zp, pltpu.roll(m, 1, 1), 0.0)
                nb = (xn + xp) + (yn + yp) + (zn + zp)
                dx = RH * (xn - xp)
                dy = RH * (yn - yp)
                if k == 0:
                    add(0, d_up * m - 0.5 * nb)
                    add(2, bx * m - dx)
                    add(3, by * m - dy)
                elif k == 1:
                    add(1, d_up * m - 0.5 * nb)
                    add(2, dy - by * m)
                    add(3, bx * m - dx)
                elif k == 2:
                    add(2, d_dn * m - 0.5 * nb)
                    add(0, bx * m + dx)
                    add(1, -(by * m) - dy)
                else:
                    add(3, d_dn * m - 0.5 * nb)
                    add(0, by * m + dy)
                    add(1, bx * m + dx)
            return o

        def run_stage(src, dst, prev, q_lo, q_hi, alpha, beta):
            for q in range(q_lo, q_hi):
                halo_plane = q < 0 or q >= planes

                def body(r, carry, q=q, halo_plane=halo_plane):
                    rows = pl.ds(pl.multiple_of(r * 8, 8), 8)
                    o = apply(src, q, rows)
                    scale = valid_ref[q + HALO] if halo_plane else None
                    for k in range(4):
                        res = alpha * o[k]
                        if prev is not None:
                            res = res + beta * prev(q, k, rows)
                        if scale is not None:
                            res = res * scale
                        dst(q, k, rows, res)
                    return carry

                lax.fori_loop(0, rows_n, body, 0)

        def put_y1(q, k, rows, v):
            y1_ref[k, q + 2, rows, :] = v

        def put_y2(q, k, rows, v):
            y2_ref[k, q + 1, rows, :] = v

        def put_out(q, k, rows, v):
            out_ref[k, q, rows, :] = v

        run_stage(band, put_y1, None, -2, planes + 2, ALPHA1, 0.0)
        run_stage(from_y1, put_y2, band, -1, planes + 1, ALPHA2, BETA2)
        run_stage(from_y2, put_out, from_y1, 0, planes, ALPHA3, BETA3)

    return kernel


def _filter_chunk(valid, fext, lo, cur_full, hi, acc, c, planes, chunk):
    aliased = acc is not None
    nb_full = cur_full.shape[2]
    rows = 8
    steps = chunk // rows
    base = c * steps
    blk = (4, HALO, rows, CELLS)
    in_specs = [
        pl.BlockSpec(memory_space=pltpu.SMEM),
        pl.BlockSpec(fext.shape, lambda i: (0, 0, 0)),
        pl.BlockSpec(blk, lambda i: (0, 0, i, 0)),
        pl.BlockSpec((4, planes, rows, CELLS), lambda i: (0, 0, base + i, 0)),
        pl.BlockSpec(blk, lambda i: (0, 0, i, 0)),
    ]
    args = [valid, fext, lo, cur_full, hi]
    extra = {}
    if aliased:
        in_specs.append(pl.BlockSpec(memory_space=pl.ANY))
        args.append(acc)
        extra["input_output_aliases"] = {5: 0}
    return pl.pallas_call(
        _make_kernel(planes, rows, aliased),
        grid=(steps,),
        in_specs=in_specs,
        out_specs=pl.BlockSpec((4, planes, rows, CELLS), lambda i: (0, 0, base + i, 0)),
        out_shape=jax.ShapeDtypeStruct((4, planes, nb_full, CELLS), jnp.float32),
        scratch_shapes=[
            pltpu.VMEM((4, planes + 4, rows, CELLS), jnp.float32),
            pltpu.VMEM((4, planes + 2, rows, CELLS), jnp.float32),
        ],
        compiler_params=pltpu.CompilerParams(vmem_limit_bytes=48 * 1024 * 1024),
        **extra,
    )(*args)


def _shift(x, axis, step):
    count = lax.axis_size(axis)
    if step > 0:
        pairs = [(i, i + 1) for i in range(count - 1)]
    else:
        pairs = [(i + 1, i) for i in range(count - 1)]
    return lax.ppermute(x, axis, pairs)


def _fields(potential, domain_blocks, block_slots, domain_offsets, held):
    ndom = lax.axis_size("dom")
    per_dev = potential.shape[2]
    d = lax.axis_index("dom")
    pot = jnp.concatenate(
        [_shift(potential[:, -2:], "grid", 1), potential, _shift(potential[:, :2], "grid", -1)], axis=1
    )
    planes = pot.shape[1]
    slot_of = block_slots[domain_blocks]
    owner = slot_of // per_dev
    locs = jnp.sum(jnp.where(owner == d, slot_of % per_dev, 0), axis=1)
    sends = jnp.moveaxis(jnp.take(pot, locs, axis=2), 2, 0)
    sends, held = lax.optimization_barrier((sends, held))
    allr = lax.all_to_all(sends, "dom", 0, 0, tiled=True)
    blocks = jnp.take(allr, lax.dynamic_index_in_dim(owner, d, 0, keepdims=False), axis=0)
    window = jnp.transpose(blocks, (1, 2, 0, 3)).reshape(4, planes, OVL * pot.shape[3])
    f = lax.dynamic_slice_in_dim(window, domain_offsets[d] * DZ, CELLS, 2)
    v, bx, by, bz = f[0], f[1], f[2], f[3]
    return jnp.stack([v + bz + (3.0 - centre), v - bz + (3.0 - centre), bx, by]), held


def per_device(bands, potential, domain_blocks, block_slots, domain_offsets):
    b = jnp.transpose(bands[0], (0, 2, 1, 3))
    planes = b.shape[1]
    nbands = b.shape[2]
    g = lax.axis_index("grid")
    ng = lax.axis_size("grid")
    chunk = CHUNK

    fext, b = _fields(potential, domain_blocks, block_slots, domain_offsets, b)

    los, his = [], []
    for c in range(nbands // chunk):
        src, _ = lax.optimization_barrier((b, g + c))
        bc = src[:, :, c * chunk : (c + 1) * chunk]
        los.append(_shift(bc[:, planes - HALO :], "grid", 1))
        his.append(_shift(bc[:, :HALO], "grid", -1))

    q = jnp.arange(-HALO, planes + HALO)
    glob = g * planes + q
    valid = ((glob >= 0) & (glob < ng * planes)).astype(jnp.float32)

    acc = None
    for c in range(nbands // chunk):
        acc = _filter_chunk(valid, fext, los[c], b, his[c], acc, c, planes, chunk)
    return jnp.transpose(acc, (0, 2, 1, 3))[None]


def solution(mesh):
    placed = (P("dom", None, None, "grid", None), P(None, "grid", "dom", None), P(), P(), P())
    return jax.shard_map(
        per_device,
        mesh=mesh,
        in_specs=placed,
        out_specs=P("dom", None, None, "grid", None),
        check_vma=False,
    )
```

```python
import jax
import jax.numpy as jnp
from jax import lax
from jax.experimental import pallas as pl
from jax.experimental.pallas import tpu as pltpu
from jax.sharding import PartitionSpec as P

DZ = 64
OVL = 6
CELLS = 1280
HALO = 3
CHUNK = 16


e_half = 4.5
centre = 5.0
sigma_one = e_half / (-3.5 - centre)
sigma_two = 1.0 / (2.0 / sigma_one - sigma_one)
sigma_three = 1.0 / (2.0 / sigma_one - sigma_two)
rashba = 0.3

ALPHA1 = sigma_one / e_half
ALPHA2 = 2.0 * sigma_two / e_half
BETA2 = -sigma_one * sigma_two
ALPHA3 = 2.0 * sigma_three / e_half
BETA3 = -sigma_two * sigma_three
RH = 0.5 * rashba


def _make_kernel(planes, chunk, aliased):
    rows_n = chunk // 8

    def kernel(valid_ref, f_ref, lo_ref, cur_ref, hi_ref, *rest):
        if aliased:
            out_ref, y1_ref, y2_ref = rest[1:]
        else:
            out_ref, y1_ref, y2_ref = rest
        lane = lax.broadcasted_iota(jnp.int32, (8, 128), 1)
        low_half = lane < 64
        z_top = lane % DZ == DZ - 1
        z_bottom = lane % DZ == 0
        tiles = CELLS // 128

        def shifted(m):
            t = [m[:, 128 * j : 128 * (j + 1)] for j in range(tiles)]
            h = [pltpu.roll(x, 64, 1) for x in t]
            yn = [jnp.where(low_half, h[j], h[j + 1]) for j in range(tiles - 1)]
            yn.append(jnp.where(low_half, h[-1], 0.0))
            yp = [jnp.where(low_half, 0.0, h[0])]
            yp += [jnp.where(low_half, h[j - 1], h[j]) for j in range(1, tiles)]
            zn = [jnp.where(z_top, 0.0, pltpu.roll(x, 127, 1)) for x in t]
            zp = [jnp.where(z_bottom, 0.0, pltpu.roll(x, 1, 1)) for x in t]
            cat = lambda parts: jnp.concatenate(parts, axis=1)
            return cat(yn), cat(yp), cat(zn), cat(zp)

        def band(q, k, rows):
            if q < 0:
                return lo_ref[k, q + HALO, rows, :]
            if q < planes:
                return cur_ref[k, q, rows, :]
            return hi_ref[k, q - planes, rows, :]

        def from_y1(q, k, rows):
            return y1_ref[k, q + 2, rows, :]

        def from_y2(q, k, rows):
            return y2_ref[k, q + 1, rows, :]

        def apply(src, q, rows):
            d_up = f_ref[0, q + 2 : q + 3, :]
            d_dn = f_ref[1, q + 2 : q + 3, :]
            bx = f_ref[2, q + 2 : q + 3, :]
            by = f_ref[3, q + 2 : q + 3, :]
            o = [None] * 4

            def add(i, v):
                o[i] = v if o[i] is None else o[i] + v

            for k in range(4):
                m = src(q, k, rows)
                xn = src(q + 1, k, rows)
                xp = src(q - 1, k, rows)
                yn, yp, zn, zp = shifted(m)
                nb = (xn + xp) + (yn + yp) + (zn + zp)
                dx = RH * (xn - xp)
                dy = RH * (yn - yp)
                if k == 0:
                    add(0, d_up * m - 0.5 * nb)
                    add(2, bx * m - dx)
                    add(3, by * m - dy)
                elif k == 1:
                    add(1, d_up * m - 0.5 * nb)
                    add(2, dy - by * m)
                    add(3, bx * m - dx)
                elif k == 2:
                    add(2, d_dn * m - 0.5 * nb)
                    add(0, bx * m + dx)
                    add(1, -(by * m) - dy)
                else:
                    add(3, d_dn * m - 0.5 * nb)
                    add(0, by * m + dy)
                    add(1, bx * m + dx)
            return o

        def run_stage(src, dst, prev, q_lo, q_hi, alpha, beta):
            for q in range(q_lo, q_hi):
                halo_plane = q < 0 or q >= planes

                def body(r, carry, q=q, halo_plane=halo_plane):
                    rows = pl.ds(pl.multiple_of(r * 8, 8), 8)
                    o = apply(src, q, rows)
                    scale = valid_ref[q + HALO] if halo_plane else None
                    for k in range(4):
                        res = alpha * o[k]
                        if prev is not None:
                            res = res + beta * prev(q, k, rows)
                        if scale is not None:
                            res = res * scale
                        dst(q, k, rows, res)
                    return carry

                lax.fori_loop(0, rows_n, body, 0)

        def put_y1(q, k, rows, v):
            y1_ref[k, q + 2, rows, :] = v

        def put_y2(q, k, rows, v):
            y2_ref[k, q + 1, rows, :] = v

        def put_out(q, k, rows, v):
            out_ref[k, q, rows, :] = v

        run_stage(band, put_y1, None, -2, planes + 2, ALPHA1, 0.0)
        run_stage(from_y1, put_y2, band, -1, planes + 1, ALPHA2, BETA2)
        run_stage(from_y2, put_out, from_y1, 0, planes, ALPHA3, BETA3)

    return kernel


def _filter_chunk(valid, fext, lo, cur_full, hi, acc, c, planes, chunk):
    aliased = acc is not None
    nb_full = cur_full.shape[2]
    rows = 8
    steps = chunk // rows
    base = c * steps
    blk = (4, HALO, rows, CELLS)
    in_specs = [
        pl.BlockSpec(memory_space=pltpu.SMEM),
        pl.BlockSpec(fext.shape, lambda i: (0, 0, 0)),
        pl.BlockSpec(blk, lambda i: (0, 0, i, 0)),
        pl.BlockSpec((4, planes, rows, CELLS), lambda i: (0, 0, base + i, 0)),
        pl.BlockSpec(blk, lambda i: (0, 0, i, 0)),
    ]
    args = [valid, fext, lo, cur_full, hi]
    extra = {}
    if aliased:
        in_specs.append(pl.BlockSpec(memory_space=pl.ANY))
        args.append(acc)
        extra["input_output_aliases"] = {5: 0}
    return pl.pallas_call(
        _make_kernel(planes, rows, aliased),
        grid=(steps,),
        in_specs=in_specs,
        out_specs=pl.BlockSpec((4, planes, rows, CELLS), lambda i: (0, 0, base + i, 0)),
        out_shape=jax.ShapeDtypeStruct((4, planes, nb_full, CELLS), jnp.float32),
        scratch_shapes=[
            pltpu.VMEM((4, planes + 4, rows, CELLS), jnp.float32),
            pltpu.VMEM((4, planes + 2, rows, CELLS), jnp.float32),
        ],
        compiler_params=pltpu.CompilerParams(vmem_limit_bytes=48 * 1024 * 1024),
        **extra,
    )(*args)


def _shift(x, axis, step):
    count = lax.axis_size(axis)
    if step > 0:
        pairs = [(i, i + 1) for i in range(count - 1)]
    else:
        pairs = [(i + 1, i) for i in range(count - 1)]
    return lax.ppermute(x, axis, pairs)


def _fields(potential, domain_blocks, block_slots, domain_offsets, held):
    ndom = lax.axis_size("dom")
    per_dev = potential.shape[2]
    d = lax.axis_index("dom")
    pot = jnp.concatenate(
        [_shift(potential[:, -2:], "grid", 1), potential, _shift(potential[:, :2], "grid", -1)], axis=1
    )
    planes = pot.shape[1]
    slot_of = block_slots[domain_blocks]
    owner = slot_of // per_dev
    locs = jnp.sum(jnp.where(owner == d, slot_of % per_dev, 0), axis=1)
    sends = jnp.moveaxis(jnp.take(pot, locs, axis=2), 2, 0)
    sends, held = lax.optimization_barrier((sends, held))
    allr = lax.all_to_all(sends, "dom", 0, 0, tiled=True)
    blocks = jnp.take(allr, lax.dynamic_index_in_dim(owner, d, 0, keepdims=False), axis=0)
    window = jnp.transpose(blocks, (1, 2, 0, 3)).reshape(4, planes, OVL * pot.shape[3])
    f = lax.dynamic_slice_in_dim(window, domain_offsets[d] * DZ, CELLS, 2)
    v, bx, by, bz = f[0], f[1], f[2], f[3]
    return jnp.stack([v + bz + (3.0 - centre), v - bz + (3.0 - centre), bx, by]), held


def per_device(bands, potential, domain_blocks, block_slots, domain_offsets):
    b = jnp.transpose(bands[0], (0, 2, 1, 3))
    planes = b.shape[1]
    nbands = b.shape[2]
    g = lax.axis_index("grid")
    ng = lax.axis_size("grid")
    chunk = CHUNK

    fext, b = _fields(potential, domain_blocks, block_slots, domain_offsets, b)

    los, his = [], []
    for c in range(nbands // chunk):
        bc = b[:, :, c * chunk : (c + 1) * chunk]
        los.append(_shift(bc[:, planes - HALO :], "grid", 1))
        his.append(_shift(bc[:, :HALO], "grid", -1))

    q = jnp.arange(-HALO, planes + HALO)
    glob = g * planes + q
    valid = ((glob >= 0) & (glob < ng * planes)).astype(jnp.float32)

    acc = None
    for c in range(nbands // chunk):
        acc = _filter_chunk(valid, fext, los[c], b, his[c], acc, c, planes, chunk)
    return jnp.transpose(acc, (0, 2, 1, 3))[None]


def solution(mesh):
    placed = (P("dom", None, None, "grid", None), P(None, "grid", "dom", None), P(), P(), P())
    return jax.shard_map(
        per_device,
        mesh=mesh,
        in_specs=placed,
        out_specs=P("dom", None, None, "grid", None),
        check_vma=False,
    )
```

```python
import jax
import jax.numpy as jnp
from jax import lax
from jax.experimental import pallas as pl
from jax.experimental.pallas import tpu as pltpu
from jax.sharding import PartitionSpec as P


DZ = 64
OVL = 6
CELLS = 1280
HALO = 3
CHUNKS = (16, 24, 24)


e_half = 4.5
centre = 5.0
sigma_one = e_half / (-3.5 - centre)
sigma_two = 1.0 / (2.0 / sigma_one - sigma_one)
sigma_three = 1.0 / (2.0 / sigma_one - sigma_two)
rashba = 0.3

ALPHA1 = sigma_one / e_half
ALPHA2 = 2.0 * sigma_two / e_half
BETA2 = -sigma_one * sigma_two
ALPHA3 = 2.0 * sigma_three / e_half
BETA3 = -sigma_two * sigma_three
RH = 0.5 * rashba


def _make_kernel(planes, chunk, aliased):
    rows_n = chunk // 8

    def kernel(valid_ref, f_ref, lo_ref, cur_ref, hi_ref, *rest):
        if aliased:
            out_ref, y1_ref, y2_ref = rest[1:]
        else:
            out_ref, y1_ref, y2_ref = rest
        lane = lax.broadcasted_iota(jnp.int32, (8, 128), 1)
        low_half = lane < 64
        z_top = lane % DZ == DZ - 1
        z_bottom = lane % DZ == 0
        tiles = CELLS // 128

        def shifted(m):
            t = [m[:, 128 * j : 128 * (j + 1)] for j in range(tiles)]
            h = [pltpu.roll(x, 64, 1) for x in t]
            yn = [jnp.where(low_half, h[j], h[j + 1]) for j in range(tiles - 1)]
            yn.append(jnp.where(low_half, h[-1], 0.0))
            yp = [jnp.where(low_half, 0.0, h[0])]
            yp += [jnp.where(low_half, h[j - 1], h[j]) for j in range(1, tiles)]
            zn = [jnp.where(z_top, 0.0, pltpu.roll(x, 127, 1)) for x in t]
            zp = [jnp.where(z_bottom, 0.0, pltpu.roll(x, 1, 1)) for x in t]
            cat = lambda parts: jnp.concatenate(parts, axis=1)
            return cat(yn), cat(yp), cat(zn), cat(zp)

        def band(q, k, rows):
            if q < 0:
                return lo_ref[k, q + HALO, rows, :]
            if q < planes:
                return cur_ref[k, q, rows, :]
            return hi_ref[k, q - planes, rows, :]

        def from_y1(q, k, rows):
            return y1_ref[k, q + 2, rows, :]

        def from_y2(q, k, rows):
            return y2_ref[k, q + 1, rows, :]

        def apply(src, q, rows):
            d_up = f_ref[0, q + 2 : q + 3, :]
            d_dn = f_ref[1, q + 2 : q + 3, :]
            bx = f_ref[2, q + 2 : q + 3, :]
            by = f_ref[3, q + 2 : q + 3, :]
            o = [None] * 4

            def add(i, v):
                o[i] = v if o[i] is None else o[i] + v

            for k in range(4):
                m = src(q, k, rows)
                xn = src(q + 1, k, rows)
                xp = src(q - 1, k, rows)
                yn, yp, zn, zp = shifted(m)
                nb = (xn + xp) + (yn + yp) + (zn + zp)
                dx = RH * (xn - xp)
                dy = RH * (yn - yp)
                if k == 0:
                    add(0, d_up * m - 0.5 * nb)
                    add(2, bx * m - dx)
                    add(3, by * m - dy)
                elif k == 1:
                    add(1, d_up * m - 0.5 * nb)
                    add(2, dy - by * m)
                    add(3, bx * m - dx)
                elif k == 2:
                    add(2, d_dn * m - 0.5 * nb)
                    add(0, bx * m + dx)
                    add(1, -(by * m) - dy)
                else:
                    add(3, d_dn * m - 0.5 * nb)
                    add(0, by * m + dy)
                    add(1, bx * m + dx)
            return o

        def run_stage(src, dst, prev, q_lo, q_hi, alpha, beta):
            for q in range(q_lo, q_hi):
                halo_plane = q < 0 or q >= planes

                def body(r, carry, q=q, halo_plane=halo_plane):
                    rows = pl.ds(pl.multiple_of(r * 8, 8), 8)
                    o = apply(src, q, rows)
                    scale = valid_ref[q + HALO] if halo_plane else None
                    for k in range(4):
                        res = alpha * o[k]
                        if prev is not None:
                            res = res + beta * prev(q, k, rows)
                        if scale is not None:
                            res = res * scale
                        dst(q, k, rows, res)
                    return carry

                lax.fori_loop(0, rows_n, body, 0)

        def put_y1(q, k, rows, v):
            y1_ref[k, q + 2, rows, :] = v

        def put_y2(q, k, rows, v):
            y2_ref[k, q + 1, rows, :] = v

        def put_out(q, k, rows, v):
            out_ref[k, q, rows, :] = v

        run_stage(band, put_y1, None, -2, planes + 2, ALPHA1, 0.0)
        run_stage(from_y1, put_y2, band, -1, planes + 1, ALPHA2, BETA2)
        run_stage(from_y2, put_out, from_y1, 0, planes, ALPHA3, BETA3)

    return kernel


def _filter_chunk(valid, fext, lo, cur_full, hi, acc, first, planes, chunk):
    aliased = acc is not None
    nb_full = cur_full.shape[2]
    rows = 8
    steps = chunk // rows
    base = first // rows
    blk = (4, HALO, rows, CELLS)
    in_specs = [
        pl.BlockSpec(memory_space=pltpu.SMEM),
        pl.BlockSpec(fext.shape, lambda i: (0, 0, 0)),
        pl.BlockSpec(blk, lambda i: (0, 0, i, 0)),
        pl.BlockSpec((4, planes, rows, CELLS), lambda i: (0, 0, base + i, 0)),
        pl.BlockSpec(blk, lambda i: (0, 0, i, 0)),
    ]
    args = [valid, fext, lo, cur_full, hi]
    extra = {}
    if aliased:
        in_specs.append(pl.BlockSpec(memory_space=pl.ANY))
        args.append(acc)
        extra["input_output_aliases"] = {5: 0}
    return pl.pallas_call(
        _make_kernel(planes, rows, aliased),
        grid=(steps,),
        in_specs=in_specs,
        out_specs=pl.BlockSpec((4, planes, rows, CELLS), lambda i: (0, 0, base + i, 0)),
        out_shape=jax.ShapeDtypeStruct((4, planes, nb_full, CELLS), jnp.float32),
        scratch_shapes=[
            pltpu.VMEM((4, planes + 4, rows, CELLS), jnp.float32),
            pltpu.VMEM((4, planes + 2, rows, CELLS), jnp.float32),
        ],
        compiler_params=pltpu.CompilerParams(vmem_limit_bytes=48 * 1024 * 1024),
        **extra,
    )(*args)


def _shift(x, axis, step):
    count = lax.axis_size(axis)
    if step > 0:
        pairs = [(i, i + 1) for i in range(count - 1)]
    else:
        pairs = [(i + 1, i) for i in range(count - 1)]
    return lax.ppermute(x, axis, pairs)


def _fields(potential, domain_blocks, block_slots, domain_offsets, held):
    per_dev = potential.shape[2]
    d = lax.axis_index("dom")
    pot = jnp.concatenate(
        [_shift(potential[:, -2:], "grid", 1), potential, _shift(potential[:, :2], "grid", -1)], axis=1
    )
    planes = pot.shape[1]
    slot_of = block_slots[domain_blocks]
    owner = slot_of // per_dev
    locs = jnp.sum(jnp.where(owner == d, slot_of % per_dev, 0), axis=1)
    sends = jnp.moveaxis(jnp.take(pot, locs, axis=2), 2, 0)
    sends, held = lax.optimization_barrier((sends, held))
    allr = lax.all_to_all(sends, "dom", 0, 0, tiled=True)
    blocks = jnp.take(allr, lax.dynamic_index_in_dim(owner, d, 0, keepdims=False), axis=0)
    window = jnp.transpose(blocks, (1, 2, 0, 3)).reshape(4, planes, OVL * pot.shape[3])
    f = lax.dynamic_slice_in_dim(window, domain_offsets[d] * DZ, CELLS, 2)
    v, bx, by, bz = f[0], f[1], f[2], f[3]
    return jnp.stack([v + bz + (3.0 - centre), v - bz + (3.0 - centre), bx, by]), held


def _per_device(bands, potential, domain_blocks, block_slots, domain_offsets):
    b = jnp.transpose(bands[0], (0, 2, 1, 3))
    planes = b.shape[1]
    g = lax.axis_index("grid")
    ng = lax.axis_size("grid")
    firsts = [sum(CHUNKS[:i]) for i in range(len(CHUNKS))]

    fext, b = _fields(potential, domain_blocks, block_slots, domain_offsets, b)

    los, his = [], []
    for first, chunk in zip(firsts, CHUNKS):
        bc = b[:, :, first : first + chunk]
        los.append(_shift(bc[:, planes - HALO :], "grid", 1))
        his.append(_shift(bc[:, :HALO], "grid", -1))

    q = jnp.arange(-HALO, planes + HALO)
    glob = g * planes + q
    valid = ((glob >= 0) & (glob < ng * planes)).astype(jnp.float32)

    acc = None
    for c, (first, chunk) in enumerate(zip(firsts, CHUNKS)):
        acc = _filter_chunk(valid, fext, los[c], b, his[c], acc, first, planes, chunk)
    return jnp.transpose(acc, (0, 2, 1, 3))[None]


def solution(mesh):
    placed = (P("dom", None, None, "grid", None), P(None, "grid", "dom", None), P(), P(), P())
    return jax.shard_map(
        _per_device,
        mesh=mesh,
        in_specs=placed,
        out_specs=P("dom", None, None, "grid", None),
        check_vma=False,
    )
```

```python
import jax
import jax.numpy as jnp
from jax import lax
from jax.experimental import pallas as pl
from jax.experimental.pallas import tpu as pltpu
from jax.sharding import PartitionSpec as P

DZ = 64
OVL = 6
CELLS = 1280
HALO = 3
CHUNK = 16


e_half = 4.5
centre = 5.0
sigma_one = e_half / (-3.5 - centre)
sigma_two = 1.0 / (2.0 / sigma_one - sigma_one)
sigma_three = 1.0 / (2.0 / sigma_one - sigma_two)
rashba = 0.3

ALPHA1 = sigma_one / e_half
ALPHA2 = 2.0 * sigma_two / e_half
BETA2 = -sigma_one * sigma_two
ALPHA3 = 2.0 * sigma_three / e_half
BETA3 = -sigma_two * sigma_three
RH = 0.5 * rashba


def _make_kernel(planes, chunk, aliased):
    rows_n = chunk // 8

    def kernel(valid_ref, f_ref, lo_ref, cur_ref, hi_ref, *rest):
        if aliased:
            out_ref, y1_ref, y2_ref = rest[1:]
        else:
            out_ref, y1_ref, y2_ref = rest
        lane = lax.broadcasted_iota(jnp.int32, (8, 128), 1)
        low_half = lane < 64
        z_top = lane % DZ == DZ - 1
        z_bottom = lane % DZ == 0
        tiles = CELLS // 128

        def shifted(m):
            t = [m[:, 128 * j : 128 * (j + 1)] for j in range(tiles)]
            h = [pltpu.roll(x, 64, 1) for x in t]
            yn = [jnp.where(low_half, h[j], h[j + 1]) for j in range(tiles - 1)]
            yn.append(jnp.where(low_half, h[-1], 0.0))
            yp = [jnp.where(low_half, 0.0, h[0])]
            yp += [jnp.where(low_half, h[j - 1], h[j]) for j in range(1, tiles)]
            zn = [jnp.where(z_top, 0.0, pltpu.roll(x, 127, 1)) for x in t]
            zp = [jnp.where(z_bottom, 0.0, pltpu.roll(x, 1, 1)) for x in t]
            cat = lambda parts: jnp.concatenate(parts, axis=1)
            return cat(yn), cat(yp), cat(zn), cat(zp)

        def band(q, k, rows):
            if q < 0:
                return lo_ref[k, q + HALO, rows, :]
            if q < planes:
                return cur_ref[k, q, rows, :]
            return hi_ref[k, q - planes, rows, :]

        def from_y1(q, k, rows):
            return y1_ref[k, q + 2, rows, :]

        def from_y2(q, k, rows):
            return y2_ref[k, q + 1, rows, :]

        def apply(src, q, rows):
            d_up = f_ref[0, q + 2 : q + 3, :]
            d_dn = f_ref[1, q + 2 : q + 3, :]
            bx = f_ref[2, q + 2 : q + 3, :]
            by = f_ref[3, q + 2 : q + 3, :]
            o = [None] * 4

            def add(i, v):
                o[i] = v if o[i] is None else o[i] + v

            for k in range(4):
                m = src(q, k, rows)
                xn = src(q + 1, k, rows)
                xp = src(q - 1, k, rows)
                yn, yp, zn, zp = shifted(m)
                nb = (xn + xp) + (yn + yp) + (zn + zp)
                dx = RH * (xn - xp)
                dy = RH * (yn - yp)
                if k == 0:
                    add(0, d_up * m - 0.5 * nb)
                    add(2, bx * m - dx)
                    add(3, by * m - dy)
                elif k == 1:
                    add(1, d_up * m - 0.5 * nb)
                    add(2, dy - by * m)
                    add(3, bx * m - dx)
                elif k == 2:
                    add(2, d_dn * m - 0.5 * nb)
                    add(0, bx * m + dx)
                    add(1, -(by * m) - dy)
                else:
                    add(3, d_dn * m - 0.5 * nb)
                    add(0, by * m + dy)
                    add(1, bx * m + dx)
            return o

        def run_stage(src, dst, prev, q_lo, q_hi, alpha, beta):
            for q in range(q_lo, q_hi):
                halo_plane = q < 0 or q >= planes

                def body(r, carry, q=q, halo_plane=halo_plane):
                    rows = pl.ds(pl.multiple_of(r * 8, 8), 8)
                    o = apply(src, q, rows)
                    scale = valid_ref[q + HALO] if halo_plane else None
                    for k in range(4):
                        res = alpha * o[k]
                        if prev is not None:
                            res = res + beta * prev(q, k, rows)
                        if scale is not None:
                            res = res * scale
                        dst(q, k, rows, res)
                    return carry

                lax.fori_loop(0, rows_n, body, 0)

        def put_y1(q, k, rows, v):
            y1_ref[k, q + 2, rows, :] = v

        def put_y2(q, k, rows, v):
            y2_ref[k, q + 1, rows, :] = v

        def put_out(q, k, rows, v):
            out_ref[k, q, rows, :] = v

        run_stage(band, put_y1, None, -2, planes + 2, ALPHA1, 0.0)
        run_stage(from_y1, put_y2, band, -1, planes + 1, ALPHA2, BETA2)
        run_stage(from_y2, put_out, from_y1, 0, planes, ALPHA3, BETA3)

    return kernel


def _filter_chunk(valid, fext, lo, cur, hi, acc, c, planes, chunk, nb_full):
    aliased = acc is not None
    rows = 8
    steps = chunk // rows
    base = c * steps
    blk = (4, HALO, rows, CELLS)
    in_specs = [
        pl.BlockSpec(memory_space=pltpu.SMEM),
        pl.BlockSpec(fext.shape, lambda i: (0, 0, 0)),
        pl.BlockSpec(blk, lambda i: (0, 0, i, 0)),
        pl.BlockSpec((4, planes, rows, CELLS), lambda i: (0, 0, i, 0)),
        pl.BlockSpec(blk, lambda i: (0, 0, i, 0)),
    ]
    args = [valid, fext, lo, cur, hi]
    extra = {}
    if aliased:
        in_specs.append(pl.BlockSpec(memory_space=pl.ANY))
        args.append(acc)
        extra["input_output_aliases"] = {5: 0}
    return pl.pallas_call(
        _make_kernel(planes, rows, aliased),
        grid=(steps,),
        in_specs=in_specs,
        out_specs=pl.BlockSpec((4, planes, rows, CELLS), lambda i: (0, 0, base + i, 0)),
        out_shape=jax.ShapeDtypeStruct((4, planes, nb_full, CELLS), jnp.float32),
        scratch_shapes=[
            pltpu.VMEM((4, planes + 4, rows, CELLS), jnp.float32),
            pltpu.VMEM((4, planes + 2, rows, CELLS), jnp.float32),
        ],
        compiler_params=pltpu.CompilerParams(vmem_limit_bytes=48 * 1024 * 1024),
        **extra,
    )(*args)


def _shift(x, axis, step):
    count = lax.axis_size(axis)
    if step > 0:
        pairs = [(i, i + 1) for i in range(count - 1)]
    else:
        pairs = [(i + 1, i) for i in range(count - 1)]
    return lax.ppermute(x, axis, pairs)


def _fields(potential, domain_blocks, block_slots, domain_offsets, held):
    ndom = lax.axis_size("dom")
    per_dev = potential.shape[2]
    d = lax.axis_index("dom")
    pot = jnp.concatenate(
        [_shift(potential[:, -2:], "grid", 1), potential, _shift(potential[:, :2], "grid", -1)], axis=1
    )
    planes = pot.shape[1]
    slot_of = block_slots[domain_blocks]
    owner = slot_of // per_dev
    locs = jnp.sum(jnp.where(owner == d, slot_of % per_dev, 0), axis=1)
    sends = jnp.moveaxis(jnp.take(pot, locs, axis=2), 2, 0)
    sends, held = lax.optimization_barrier((sends, held))
    allr = lax.all_to_all(sends, "dom", 0, 0, tiled=True)
    blocks = jnp.take(allr, lax.dynamic_index_in_dim(owner, d, 0, keepdims=False), axis=0)
    window = jnp.transpose(blocks, (1, 2, 0, 3)).reshape(4, planes, OVL * pot.shape[3])
    f = lax.dynamic_slice_in_dim(window, domain_offsets[d] * DZ, CELLS, 2)
    v, bx, by, bz = f[0], f[1], f[2], f[3]
    return jnp.stack([v + bz + (3.0 - centre), v - bz + (3.0 - centre), bx, by]), held


def per_device(bands, potential, domain_blocks, block_slots, domain_offsets):
    b = jnp.transpose(bands[0], (0, 2, 1, 3))
    planes = b.shape[1]
    nbands = b.shape[2]
    g = lax.axis_index("grid")
    ng = lax.axis_size("grid")
    chunk = CHUNK

    fext, b = _fields(potential, domain_blocks, block_slots, domain_offsets, b)

    los, his, bcs = [], [], []
    for c in range(nbands // chunk):
        bc = b[:, :, c * chunk : (c + 1) * chunk]
        bcs.append(bc)
        los.append(_shift(bc[:, planes - HALO :], "grid", 1))
        his.append(_shift(bc[:, :HALO], "grid", -1))

    q = jnp.arange(-HALO, planes + HALO)
    glob = g * planes + q
    valid = ((glob >= 0) & (glob < ng * planes)).astype(jnp.float32)

    acc = None
    for c in range(nbands // chunk):
        acc = _filter_chunk(valid, fext, los[c], bcs[c], his[c], acc, c, planes, chunk, nbands)
    return jnp.transpose(acc, (0, 2, 1, 3))[None]


def solution(mesh):
    placed = (P("dom", None, None, "grid", None), P(None, "grid", "dom", None), P(), P(), P())
    return jax.shard_map(
        per_device,
        mesh=mesh,
        in_specs=placed,
        out_specs=P("dom", None, None, "grid", None),
        check_vma=False,
    )
```

```python
import jax
import jax.numpy as jnp
from jax import lax
from jax.experimental import pallas as pl
from jax.experimental.pallas import tpu as pltpu
from jax.sharding import PartitionSpec as P

DZ = 64
OVL = 6
CELLS = 1280
HALO = 3
CHUNK = 16


e_half = 4.5
centre = 5.0
sigma_one = e_half / (-3.5 - centre)
sigma_two = 1.0 / (2.0 / sigma_one - sigma_one)
sigma_three = 1.0 / (2.0 / sigma_one - sigma_two)
rashba = 0.3

ALPHA1 = sigma_one / e_half
ALPHA2 = 2.0 * sigma_two / e_half
BETA2 = -sigma_one * sigma_two
ALPHA3 = 2.0 * sigma_three / e_half
BETA3 = -sigma_two * sigma_three
RH = 0.5 * rashba
SCALES = (ALPHA1, ALPHA2, ALPHA3)


def _make_kernel(planes, chunk, aliased):
    rows_n = chunk // 8

    def kernel(valid_ref, f_ref, lo_ref, cur_ref, hi_ref, *rest):
        if aliased:
            out_ref, y1_ref, y2_ref = rest[1:]
        else:
            out_ref, y1_ref, y2_ref = rest
        lane = lax.broadcasted_iota(jnp.int32, (8, 128), 1)
        low_half = lane < 64
        z_top = lane % DZ == DZ - 1
        z_bottom = lane % DZ == 0
        tiles = CELLS // 128

        def shifted(m):
            t = [m[:, 128 * j : 128 * (j + 1)] for j in range(tiles)]
            h = [pltpu.roll(x, 64, 1) for x in t]
            yn = [jnp.where(low_half, h[j], h[j + 1]) for j in range(tiles - 1)]
            yn.append(jnp.where(low_half, h[-1], 0.0))
            yp = [jnp.where(low_half, 0.0, h[0])]
            yp += [jnp.where(low_half, h[j - 1], h[j]) for j in range(1, tiles)]
            zn = [jnp.where(z_top, 0.0, pltpu.roll(x, 127, 1)) for x in t]
            zp = [jnp.where(z_bottom, 0.0, pltpu.roll(x, 1, 1)) for x in t]
            cat = lambda parts: jnp.concatenate(parts, axis=1)
            return cat(yn), cat(yp), cat(zn), cat(zp)

        def band(q, k, rows):
            if q < 0:
                return lo_ref[k, q + HALO, rows, :]
            if q < planes:
                return cur_ref[k, q, rows, :]
            return hi_ref[k, q - planes, rows, :]

        def from_y1(q, k, rows):
            return y1_ref[k, q + 2, rows, :]

        def from_y2(q, k, rows):
            return y2_ref[k, q + 1, rows, :]

        def apply(src, q, rows, st):
            d_up = f_ref[st, 0, q + 2 : q + 3, :]
            d_dn = f_ref[st, 1, q + 2 : q + 3, :]
            bx = f_ref[st, 2, q + 2 : q + 3, :]
            by = f_ref[st, 3, q + 2 : q + 3, :]
            half = -0.5 * SCALES[st]
            rh = RH * SCALES[st]
            o = [None] * 4

            def add(i, v):
                o[i] = v if o[i] is None else o[i] + v

            for k in range(4):
                m = src(q, k, rows)
                xn = src(q + 1, k, rows)
                xp = src(q - 1, k, rows)
                yn, yp, zn, zp = shifted(m)
                nb = (xn + xp) + (yn + yp) + (zn + zp)
                dx = rh * (xn - xp)
                dy = rh * (yn - yp)
                if k == 0:
                    add(0, d_up * m + half * nb)
                    add(2, bx * m - dx)
                    add(3, by * m - dy)
                elif k == 1:
                    add(1, d_up * m + half * nb)
                    add(2, dy - by * m)
                    add(3, bx * m - dx)
                elif k == 2:
                    add(2, d_dn * m + half * nb)
                    add(0, bx * m + dx)
                    add(1, -(by * m) - dy)
                else:
                    add(3, d_dn * m + half * nb)
                    add(0, by * m + dy)
                    add(1, bx * m + dx)
            return o

        def run_stage(src, dst, prev, q_lo, q_hi, st, beta):
            for q in range(q_lo, q_hi):
                halo_plane = q < 0 or q >= planes

                def body(r, carry, q=q, halo_plane=halo_plane):
                    rows = pl.ds(pl.multiple_of(r * 8, 8), 8)
                    o = apply(src, q, rows, st)
                    scale = valid_ref[q + HALO] if halo_plane else None
                    for k in range(4):
                        res = o[k]
                        if prev is not None:
                            res = res + beta * prev(q, k, rows)
                        if scale is not None:
                            res = res * scale
                        dst(q, k, rows, res)
                    return carry

                lax.fori_loop(0, rows_n, body, 0)

        def put_y1(q, k, rows, v):
            y1_ref[k, q + 2, rows, :] = v

        def put_y2(q, k, rows, v):
            y2_ref[k, q + 1, rows, :] = v

        def put_out(q, k, rows, v):
            out_ref[k, q, rows, :] = v

        run_stage(band, put_y1, None, -2, planes + 2, 0, 0.0)
        run_stage(from_y1, put_y2, band, -1, planes + 1, 1, BETA2)
        run_stage(from_y2, put_out, from_y1, 0, planes, 2, BETA3)

    return kernel


def _filter_chunk(valid, fext, lo, cur, hi, acc, c, planes, chunk, nb_full):
    aliased = acc is not None
    rows = 8
    steps = chunk // rows
    base = c * steps
    blk = (4, HALO, rows, CELLS)
    in_specs = [
        pl.BlockSpec(memory_space=pltpu.SMEM),
        pl.BlockSpec(fext.shape, lambda i: (0, 0, 0, 0)),
        pl.BlockSpec(blk, lambda i: (0, 0, i, 0)),
        pl.BlockSpec((4, planes, rows, CELLS), lambda i: (0, 0, i, 0)),
        pl.BlockSpec(blk, lambda i: (0, 0, i, 0)),
    ]
    args = [valid, fext, lo, cur, hi]
    extra = {}
    if aliased:
        in_specs.append(pl.BlockSpec(memory_space=pl.ANY))
        args.append(acc)
        extra["input_output_aliases"] = {5: 0}
    return pl.pallas_call(
        _make_kernel(planes, rows, aliased),
        grid=(steps,),
        in_specs=in_specs,
        out_specs=pl.BlockSpec((4, planes, rows, CELLS), lambda i: (0, 0, base + i, 0)),
        out_shape=jax.ShapeDtypeStruct((4, planes, nb_full, CELLS), jnp.float32),
        scratch_shapes=[
            pltpu.VMEM((4, planes + 4, rows, CELLS), jnp.float32),
            pltpu.VMEM((4, planes + 2, rows, CELLS), jnp.float32),
        ],
        compiler_params=pltpu.CompilerParams(vmem_limit_bytes=48 * 1024 * 1024),
        **extra,
    )(*args)


def _shift(x, axis, step):
    count = lax.axis_size(axis)
    if step > 0:
        pairs = [(i, i + 1) for i in range(count - 1)]
    else:
        pairs = [(i + 1, i) for i in range(count - 1)]
    return lax.ppermute(x, axis, pairs)


def _fields(potential, domain_blocks, block_slots, domain_offsets, held):
    ndom = lax.axis_size("dom")
    per_dev = potential.shape[2]
    d = lax.axis_index("dom")
    pot = jnp.concatenate(
        [_shift(potential[:, -2:], "grid", 1), potential, _shift(potential[:, :2], "grid", -1)], axis=1
    )
    planes = pot.shape[1]
    slot_of = block_slots[domain_blocks]
    owner = slot_of // per_dev
    locs = jnp.sum(jnp.where(owner == d, slot_of % per_dev, 0), axis=1)
    sends = jnp.moveaxis(jnp.take(pot, locs, axis=2), 2, 0)
    sends, held = lax.optimization_barrier((sends, held))
    allr = lax.all_to_all(sends, "dom", 0, 0, tiled=True)
    blocks = jnp.take(allr, lax.dynamic_index_in_dim(owner, d, 0, keepdims=False), axis=0)
    window = jnp.transpose(blocks, (1, 2, 0, 3)).reshape(4, planes, OVL * pot.shape[3])
    f = lax.dynamic_slice_in_dim(window, domain_offsets[d] * DZ, CELLS, 2)
    v, bx, by, bz = f[0], f[1], f[2], f[3]
    return jnp.stack([v + bz + (3.0 - centre), v - bz + (3.0 - centre), bx, by]), held


def per_device(bands, potential, domain_blocks, block_slots, domain_offsets):
    b = jnp.transpose(bands[0], (0, 2, 1, 3))
    planes = b.shape[1]
    nbands = b.shape[2]
    g = lax.axis_index("grid")
    ng = lax.axis_size("grid")
    chunk = CHUNK

    fext, b = _fields(potential, domain_blocks, block_slots, domain_offsets, b)

    los, his, bcs = [], [], []
    for c in range(nbands // chunk):
        bc = b[:, :, c * chunk : (c + 1) * chunk]
        bcs.append(bc)
        los.append(_shift(bc[:, planes - HALO :], "grid", 1))
        his.append(_shift(bc[:, :HALO], "grid", -1))

    q = jnp.arange(-HALO, planes + HALO)
    glob = g * planes + q
    valid = ((glob >= 0) & (glob < ng * planes)).astype(jnp.float32)

    fext = jnp.stack([a * fext for a in SCALES])
    acc = None
    for c in range(nbands // chunk):
        acc = _filter_chunk(valid, fext, los[c], bcs[c], his[c], acc, c, planes, chunk, nbands)
    return jnp.transpose(acc, (0, 2, 1, 3))[None]


def solution(mesh):
    placed = (P("dom", None, None, "grid", None), P(None, "grid", "dom", None), P(), P(), P())
    return jax.shard_map(
        per_device,
        mesh=mesh,
        in_specs=placed,
        out_specs=P("dom", None, None, "grid", None),
        check_vma=False,
    )
```
